512 devices in a mesh: req: 128 (over z, x, core), tp: 4 (over y).
Axes of the slice: x: 4, y: 4, z: 16, core: 2. Of those that a mesh axis runs over, the one named last changes fastest.
Arguments:
- queries: bfloat16 [16384, 3584], P('req', 'tp'), may hold values from -13 to 13
- tree_kv: bfloat16 [16384, 4, 256], P('req', 'tp'), may hold values from -5 to 5
- page_pool: bfloat16 [1536, 4, 128, 256], P('req', 'tp'), may hold values from -5 to 5
- page_table: int32 [256, 8], P('req'), may hold values from 0 to 11, as said below
- cache_len: int32 [256], P('req'), may hold values from 1 to 1024
- parents: int32 [256, 64], P('req'), may hold values from -1 to 62, as said below
- accepted: int32 [256], P('req'), may hold values from 0 to 63
- o_weight: bfloat16 [3584, 1792], P('tp'), may hold values from -0.5 to 0.5
Outputs:
- projected: bfloat16 [16384, 1792], P(('req', 'tp'))
- kept_rows: bfloat16 [16384, 4, 256], P('req', 'tp')
The draws below stay inside these ranges and needn't reach their ends.
Inputs may be any that keep to these rules, and one draw needn't show every extreme that they name: Logical page k of request r is in slot page_table[r, k] of its own device's pool for k < 2, among that pool's first 4 slots, and for k >= 2 in that slot of the next req device's pool (the first device after the last), among its last 8 slots; distinct pages are in distinct slots; entries at k >= ceil(cache_len[r] / 128) are 0. parents[r, 0] = -1 and 0 <= parents[r, j] < j for j >= 1.
All inputs are finite; a program needn't handle non-finite values.
Results may differ from the reference program's by a relative error of at most 0.007.
Values may be sent and summed in bfloat16 or wider, within the bound.
No kernel may reach another device: no remote copies, remote signals or barrier semaphores. Data moves between devices by JAX's collectives and lax.ppermute only.
A program may use at most 64 MiB of HBM per device.

```python
import math
import jax
import jax.numpy as jnp
from jax import lax

HQ = 28
KVH = 4
HEAD_SIZE = 128
D_WIN = 1792
PAGE = 128
TREE = 64
MAXP = 8
LOCAL = 2
SPILL_PAGES = 8
REQ_DEV = 2
REQS = 256
TOKENS = 16384
POOL = 12
PAGES_ALL = 1536
N_REQ = 128


def page_layout(key):
    devices = REQS // REQ_DEV
    own_slots = REQ_DEV * LOCAL
    request_ids = jnp.arange(REQ_DEV, dtype=jnp.int32)[None, :]
    device_ids = jnp.arange(devices, dtype=jnp.int32)[:, None]
    big_request = jax.random.randint(jax.random.fold_in(key, 11), (devices, 1), 0, REQ_DEV)
    big_pages = jax.random.randint(jax.random.fold_in(key, 12), (devices, 1), LOCAL + 1, MAXP + 1)
    big_pages = jnp.where(device_ids == 0, MAXP, big_pages)
    room = SPILL_PAGES - (big_pages - LOCAL)
    other_offset = jax.random.randint(jax.random.fold_in(key, 13), (devices, 1), 1, max(REQ_DEV, 2))
    second = (big_request + other_offset) % REQ_DEV
    extra = jax.random.randint(jax.random.fold_in(key, 14), (devices, 1), 0, room + 1)
    extra = jnp.minimum(extra, MAXP - LOCAL)
    small_pages = jax.random.randint(jax.random.fold_in(key, 15), (devices, REQ_DEV), 1, LOCAL + 1)
    is_second = (request_ids == second) & (second != big_request) & (extra > 0)
    pages = jnp.where(request_ids == big_request, big_pages, jnp.where(is_second, LOCAL + extra, small_pages))
    last_fill = jax.random.randint(jax.random.fold_in(key, 16), (devices, REQ_DEV), 1, PAGE + 1)
    lengths = (pages - 1) * PAGE + last_fill
    lengths = jnp.where((device_ids == 0) & (request_ids == big_request), MAXP * PAGE, lengths)
    spilled = jnp.maximum(pages - LOCAL, 0)
    before = jnp.cumsum(spilled, axis=1) - spilled
    own_perm = jax.vmap(lambda sub: jax.random.permutation(sub, own_slots))(jax.random.split(jax.random.fold_in(key, 17), devices))
    spill_perm = jax.vmap(lambda sub: jax.random.permutation(sub, SPILL_PAGES))(jax.random.split(jax.random.fold_in(key, 18), devices))
    page_ids = jnp.arange(MAXP, dtype=jnp.int32)[None, None, :]
    own_pos = request_ids[:, :, None] * LOCAL + jnp.minimum(page_ids, LOCAL - 1)
    own_pos = jnp.broadcast_to(own_pos, (devices, REQ_DEV, MAXP)).reshape(devices, REQ_DEV * MAXP)
    own_slot = jnp.take_along_axis(own_perm, own_pos, axis=1).reshape(devices, REQ_DEV, MAXP)
    spill_pos = jnp.clip(before[:, :, None] + page_ids - LOCAL, 0, SPILL_PAGES - 1).reshape(devices, REQ_DEV * MAXP)
    spill_slot = own_slots + jnp.take_along_axis(spill_perm, spill_pos, axis=1).reshape(devices, REQ_DEV, MAXP)
    table = jnp.where(page_ids < LOCAL, own_slot, spill_slot)
    table = jnp.where(page_ids < pages[:, :, None], table, 0)
    return (table.reshape(REQS, MAXP).astype(jnp.int32), lengths.reshape(REQS).astype(jnp.int32))


def draw_page_table(key, part):
    return page_layout(key)[0]


def draw_cache_len(key, part):
    return page_layout(key)[1]


def draw_parents(key, part):
    node_ids = jnp.arange(TREE, dtype=jnp.int32)[None, :]
    back_steps = jax.random.randint(key, (REQS, TREE), 0, 8)
    parent_ids = jnp.maximum(node_ids - 1 - back_steps, 0)
    return jnp.where(node_ids == 0, -1, parent_ids).astype(jnp.int32)


def key_value_block(key, shape):
    block = jax.random.normal(key, shape, jnp.float32)
    return jnp.clip(block, -5.0, 5.0).astype(jnp.bfloat16)


def draw_tree_kv(key, part):
    return key_value_block(key, (TOKENS, KVH, 2 * HEAD_SIZE))


def draw_page_pool(key, part):
    return key_value_block(key, (PAGES_ALL, KVH, PAGE, 2 * HEAD_SIZE))


def draw_queries(key, part):
    shape = (TOKENS, HQ * HEAD_SIZE)
    block = jax.random.normal(key, shape, jnp.float32)
    return jnp.clip(block, -13.0, 13.0).astype(jnp.bfloat16)


def with_ends(values, own_key, smallest, largest):
    longest = values.shape.index(max(values.shape))
    spots = []
    for shift in (0, 1):
        where = [jax.random.randint(jax.random.fold_in(own_key, axis), (), 0, length) for axis, length in enumerate(values.shape)]
        where[longest] = (where[longest] + shift) % values.shape[longest]
        spots.append(tuple(where))
    return values.at[spots[0]].set(smallest).at[spots[1]].set(largest)


def block_levels(rng, extent, cuts, low, top_value):
    loudness, own = 1.0, jax.random.fold_in(rng, 6)
    for axis_at, shards_of in cuts:
        steps = jnp.exp(jax.random.uniform(jax.random.fold_in(own, axis_at), (shards_of,), jnp.float32, low / len(cuts), top_value / len(cuts)))
        loudness = loudness * jnp.repeat(steps, extent[axis_at] // shards_of).reshape([-1 if axis == axis_at else 1 for axis in range(len(extent))])
    return loudness


def bell_draw(stream_key, shape, deviation, most, pieces=(), held_as=jnp.bfloat16):
    drawn = deviation * jax.random.normal(stream_key, shape, jnp.float32)
    if pieces:
        drawn = drawn * block_levels(stream_key, shape, pieces, -0.22, 0.18)
    return jnp.clip(drawn, -most, most).astype(held_as)


def setup_inputs(seed: int = 0) -> dict:
    key_of = jax.random.split(jax.random.key(seed), 9)
    return {
        "queries": draw_queries(jax.random.fold_in(key_of[8], 71), 0),
        "tree_kv": draw_tree_kv(jax.random.fold_in(key_of[8], 71), 0),
        "page_pool": draw_page_pool(jax.random.fold_in(key_of[8], 71), 0),
        "page_table": draw_page_table(jax.random.fold_in(key_of[8], 71), 0),
        "cache_len": draw_cache_len(jax.random.fold_in(key_of[8], 71), 0),
        "parents": draw_parents(jax.random.fold_in(key_of[8], 71), 0),
        "accepted": with_ends(jax.random.randint(key_of[6], (REQS,), 0, TREE), jax.random.fold_in(key_of[6], 1), 0, TREE - 1).astype(jnp.int32),
        "o_weight": bell_draw(key_of[7], (HQ * HEAD_SIZE, D_WIN), HEAD_SIZE ** -0.5, 0.5, ((0, 4),)),
    }


very_negative = -1e+30

def ancestors(parent_row):
    tree_len = parent_row.shape[0]
    node_ids = jnp.arange(tree_len, dtype=jnp.int32)
    parent_links = (parent_row[:, None] == node_ids[None, :]).astype(jnp.float32)
    reachable = jnp.eye(tree_len, dtype=jnp.float32) + parent_links
    for squaring in range((tree_len - 1).bit_length()):
        reachable = jnp.minimum(jnp.dot(reachable, reachable, precision=lax.Precision.HIGHEST), 1.0)
    return reachable

def reference(queries, tree_kv, page_pool, page_table, cache_len, parents, accepted, o_weight):
    group_size = HQ // KVH
    logit_scale = 1.0 / math.sqrt(HEAD_SIZE)
    query_rows = queries.reshape(REQS, TREE, KVH, group_size, HEAD_SIZE)
    tree_rows = tree_kv.reshape(REQS, TREE, KVH, 2 * HEAD_SIZE)
    home_device = jnp.arange(REQS, dtype=jnp.int32) // REQ_DEV
    page_ids = jnp.arange(MAXP, dtype=jnp.int32)
    offsets = jnp.arange(PAGE, dtype=jnp.int32)

    def one_request(request_data):
        request_query, request_draft_tree, parent_row, length, table_row, home, leaf_node = request_data
        owner_device = jnp.where(page_ids < LOCAL, home, (home + 1) % N_REQ)
        global_page = (owner_device * POOL + table_row).astype(jnp.int32)
        pages = page_pool[global_page]
        npages = (length + PAGE - 1) // PAGE
        visible = (page_ids[:, None] * PAGE + offsets[None, :] < length) & (page_ids[:, None] < npages)
        query_widened = request_query.astype(jnp.float32)
        scores = jnp.einsum('thgd,khnd->htgkn', query_widened, pages[..., :HEAD_SIZE].astype(jnp.float32)) * logit_scale
        page_mask = visible[None, None, None, :, :]
        scores = jnp.where(page_mask, scores, very_negative)
        maxima = lax.optimization_barrier(jnp.max(scores, axis=-1))
        weights = jnp.where(page_mask, jnp.exp(scores - maxima[..., None]), 0.0).astype(jnp.bfloat16)
        totals = lax.optimization_barrier(jnp.sum(weights.astype(jnp.float32), axis=-1))
        accums = jnp.einsum('htgkn,khnd->htgkd', weights.astype(jnp.float32), pages[..., HEAD_SIZE:].astype(jnp.float32))
        reachable = ancestors(parent_row)
        tree_mask = (reachable > 0.5)[None, :, None, :]
        tree_logits = jnp.einsum('qave,wae->aqvw', query_widened, request_draft_tree[..., :HEAD_SIZE].astype(jnp.float32)) * logit_scale
        tree_logits = jnp.where(tree_mask, tree_logits, very_negative)
        tree_max = lax.optimization_barrier(jnp.max(tree_logits, axis=-1))
        tree_probabilities = jnp.where(tree_mask, jnp.exp(tree_logits - tree_max[..., None]), 0.0).astype(jnp.bfloat16)
        tree_total = lax.optimization_barrier(jnp.sum(tree_probabilities.astype(jnp.float32), axis=-1))
        tree_running_sum = jnp.einsum('ieku,uiz->iekz', tree_probabilities.astype(jnp.float32), request_draft_tree[..., HEAD_SIZE:].astype(jnp.float32))
        overall = jnp.maximum(tree_max, lax.optimization_barrier(jnp.max(maxima, axis=-1)))
        page_factors = jnp.exp(maxima - overall[..., None])
        tree_factor = jnp.exp(tree_max - overall)
        numerator = lax.optimization_barrier(jnp.sum(page_factors[..., None] * accums, axis=3)) + tree_factor[..., None] * tree_running_sum
        denominator = lax.optimization_barrier(jnp.sum(page_factors * totals, axis=-1)) + tree_factor * tree_total
        normalized = (numerator / denominator[..., None]).astype(jnp.bfloat16)
        attention = jnp.transpose(normalized, (1, 0, 2, 3)).reshape(TREE, HQ * HEAD_SIZE)
        depths = lax.optimization_barrier(jnp.sum(reachable, axis=1)) - 1.0
        kept_mask = reachable[leaf_node]
        slot_ids = jnp.arange(TREE, dtype=jnp.float32)
        selector = kept_mask[None, :] * (depths[None, :] == slot_ids[:, None]).astype(jnp.float32)
        kept = jnp.einsum('sm,mhc->shc', selector, request_draft_tree.astype(jnp.float32)).astype(jnp.bfloat16)
        return (attention, kept)
    attention, kept = lax.map(one_request, (query_rows, tree_rows, parents, cache_len, page_table, home_device, accepted))
    projected = jnp.dot(attention.reshape(TOKENS, HQ * HEAD_SIZE), o_weight, preferred_element_type=jnp.float32).astype(jnp.bfloat16)
    return (projected, kept.reshape(TOKENS, KVH, 2 * HEAD_SIZE))
```

```python
import math

import jax
import jax.numpy as jnp
from jax import lax
from jax.experimental import pallas as pl
from jax.experimental.pallas import tpu as pltpu
from jax.sharding import PartitionSpec as P

HEAD_SIZE = 128
LOCAL = 2

very_negative = -1e30


def from_behind(block, axis, distance):
    devices = range(lax.axis_size(axis))
    route = [((i - distance) % len(devices), i) for i in devices]
    return lax.ppermute(block, axis, route)


def nt_dot(a, b):
    return lax.dot_general(a, b, (((1,), (1,)), ((), ())), preferred_element_type=jnp.float32)


def attention_kernel(
    table_ref, len_ref, leaf_ref, parents_ref, q_ref, tree_ref, pool_ref, spill_ref,
    att_ref, kept_ref, m_sc, l_sc, a_sc,
):
    n_req, tree_len = parents_ref.shape
    heads = q_ref.shape[1] // HEAD_SIZE
    page_len = pool_ref.shape[1]
    max_pages = table_ref.shape[1]
    spill_slots = spill_ref.shape[0]
    spill_base = pool_ref.shape[0] - spill_slots
    scale = 1.0 / math.sqrt(HEAD_SIZE)
    sub = lax.broadcasted_iota(jnp.int32, (tree_len, tree_len), 0)
    lane = lax.broadcasted_iota(jnp.int32, (tree_len, tree_len), 1)
    eye = (sub == lane).astype(jnp.float32)
    page_lane = lax.broadcasted_iota(jnp.int32, (1, page_len), 1)
    squarings = (tree_len - 1).bit_length()

    for r in range(n_req):
        rows = pl.ds(r * tree_len, tree_len)
        par = parents_ref[r : r + 1, :]
        rt = eye + (sub == par).astype(jnp.float32)
        for _ in range(squarings):
            rb = rt.astype(jnp.bfloat16)
            rt = jnp.minimum(jnp.dot(rb, rb, preferred_element_type=jnp.float32), 1.0)
        reach = nt_dot(eye.astype(jnp.bfloat16), rt.astype(jnp.bfloat16))

        depth = jnp.sum(rt, axis=0, keepdims=True) - 1.0
        leaf = leaf_ref[r]
        kept_mask = jnp.sum(jnp.where(sub == leaf, reach, 0.0), axis=0, keepdims=True)
        selector = jnp.where(
            (sub.astype(jnp.float32) == depth) & (kept_mask > 0.5), 1.0, 0.0
        ).astype(jnp.bfloat16)
        tree_rows = tree_ref[rows, :]
        kept_ref[rows, :] = jnp.dot(
            selector, tree_rows, preferred_element_type=jnp.float32
        ).astype(kept_ref.dtype)

        q = q_ref[rows, :]
        q_all = jnp.concatenate(
            [q[:, g * HEAD_SIZE : (g + 1) * HEAD_SIZE] for g in range(heads)], axis=0
        )

        tree_mask = jnp.concatenate([reach] * heads, axis=0) > 0.5
        s = nt_dot(q_all, tree_rows[:, :HEAD_SIZE]) * scale
        s = jnp.where(tree_mask, s, very_negative)
        m = jnp.max(s, axis=1, keepdims=True)
        w = jnp.where(tree_mask, jnp.exp(s - m), 0.0).astype(jnp.bfloat16)
        m_sc[...] = m
        l_sc[...] = jnp.sum(w.astype(jnp.float32), axis=1, keepdims=True)
        a_sc[...] = jnp.dot(w, tree_rows[:, HEAD_SIZE:], preferred_element_type=jnp.float32)

        length = len_ref[r]
        n_pages = (length + page_len - 1) // page_len
        for k in range(max_pages):

            @pl.when(k < n_pages)
            def _():
                slot = table_ref[r, k]
                if k < LOCAL:
                    page = pool_ref[slot]
                else:
                    page = spill_ref[jnp.clip(slot - spill_base, 0, spill_slots - 1)]
                visible = (k * page_len + page_lane) < length
                ps = nt_dot(q_all, page[:, :HEAD_SIZE]) * scale
                ps = jnp.where(visible, ps, very_negative)
                pm = jnp.max(ps, axis=1, keepdims=True)
                pw = jnp.where(visible, jnp.exp(ps - pm), 0.0).astype(jnp.bfloat16)
                pl_sum = jnp.sum(pw.astype(jnp.float32), axis=1, keepdims=True)
                pa = jnp.dot(pw, page[:, HEAD_SIZE:], preferred_element_type=jnp.float32)
                old_m = m_sc[...]
                new_m = jnp.maximum(old_m, pm)
                f_old = jnp.exp(old_m - new_m)
                f_new = jnp.exp(pm - new_m)
                m_sc[...] = new_m
                l_sc[...] = f_old * l_sc[...] + f_new * pl_sum
                a_sc[...] = f_old * a_sc[...] + f_new * pa

        att = (a_sc[...] / l_sc[...]).astype(att_ref.dtype)
        for g in range(heads):
            att_ref[rows, pl.ds(g * HEAD_SIZE, HEAD_SIZE)] = att[g * tree_len : (g + 1) * tree_len]


def shards(queries, tree_kv, page_pool, page_table, cache_len, parents, accepted, o_weight):
    requests, tree_len = parents.shape
    heads = queries.shape[1] // HEAD_SIZE
    pool_slots = page_pool[:, 0]
    own_slots = requests * LOCAL
    spill = from_behind(pool_slots[own_slots:], "req", -1)
    tree_rows = tree_kv[:, 0, :]
    smem = pl.BlockSpec(memory_space=pltpu.SMEM)
    vmem = pl.BlockSpec(memory_space=pltpu.VMEM)
    attention, kept = pl.pallas_call(
        attention_kernel,
        out_shape=(
            jax.ShapeDtypeStruct(queries.shape, jnp.bfloat16),
            jax.ShapeDtypeStruct(tree_rows.shape, jnp.bfloat16),
        ),
        in_specs=[smem, smem, smem, vmem, vmem, vmem, vmem, vmem],
        out_specs=(vmem, vmem),
        scratch_shapes=[
            pltpu.VMEM((heads * tree_len, 1), jnp.float32),
            pltpu.VMEM((heads * tree_len, 1), jnp.float32),
            pltpu.VMEM((heads * tree_len, HEAD_SIZE), jnp.float32),
        ],
    )(page_table, cache_len, accepted, parents, queries, tree_rows, pool_slots, spill)

    partial = jnp.dot(attention, o_weight, preferred_element_type=jnp.float32)
    parts = lax.axis_size("tp")
    me = lax.axis_index("tp")
    blocks = partial.reshape(parts, partial.shape[0] // parts, partial.shape[1])
    total = blocks[me]
    for shift in range(1, parts):
        outgoing = blocks[(me + shift) % parts]
        route = [(i, (i + shift) % parts) for i in range(parts)]
        total = total + lax.ppermute(outgoing, "tp", route)
    projected = total.astype(jnp.bfloat16)
    return (projected, kept.reshape(kept.shape[0], 1, kept.shape[1]))


def solution(mesh):
    in_specs = (
        P("req", "tp"),
        P("req", "tp", None),
        P("req", "tp", None, None),
        P("req", None),
        P("req"),
        P("req", None),
        P("req"),
        P("tp", None),
    )
    out_specs = (P(("req", "tp"), None), P("req", "tp", None))
    return jax.shard_map(shards, mesh=mesh, in_specs=in_specs, out_specs=out_specs, check_vma=False)
```

```python
import functools
import math

import jax
import jax.numpy as jnp
from jax import lax
from jax.experimental import pallas as pl
from jax.experimental.pallas import tpu as pltpu
from jax.sharding import PartitionSpec as P

HEAD_SIZE = 128
LOCAL = 2

very_negative = -1e30


def from_behind(block, axis, distance):
    devices = range(lax.axis_size(axis))
    route = [((i - distance) % len(devices), i) for i in devices]
    return lax.ppermute(block, axis, route)


def nt_dot(a, b):
    return lax.dot_general(a, b, (((1,), (1,)), ((), ())), preferred_element_type=jnp.float32)


def stacked_queries(q_ref, rows, heads):
    q = q_ref[rows, :]
    return jnp.concatenate(
        [q[:, g * HEAD_SIZE : (g + 1) * HEAD_SIZE] for g in range(heads)], axis=0
    )


def page_blocks(q_all, pages, first_page, length):
    page_len = pages[0].shape[0]
    keys = jnp.concatenate([page[:, :HEAD_SIZE] for page in pages], axis=0)
    lane = lax.broadcasted_iota(jnp.int32, (1, keys.shape[0]), 1)
    visible = (first_page * page_len + lane) < length
    scores = nt_dot(q_all, keys) * (1.0 / math.sqrt(HEAD_SIZE))
    scores = jnp.where(visible, scores, very_negative)
    blocks = []
    for k, page in enumerate(pages):
        cols = slice(k * page_len, (k + 1) * page_len)
        s = scores[:, cols]
        m = jnp.max(s, axis=1, keepdims=True)
        w = jnp.where(visible[:, cols], jnp.exp(s - m), 0.0).astype(jnp.bfloat16)
        l = jnp.sum(w.astype(jnp.float32), axis=1, keepdims=True)
        a = jnp.dot(w, page[:, HEAD_SIZE:], preferred_element_type=jnp.float32)
        blocks.append((m, l, a))
    return blocks


def merge(blocks):
    top = blocks[0][0]
    for m, _, _ in blocks[1:]:
        top = jnp.maximum(top, m)
    total = None
    accum = None
    for m, l, a in blocks:
        f = jnp.exp(m - top)
        total = f * l if total is None else total + f * l
        accum = f * a if accum is None else accum + f * a
    return top, total, accum


def local_kernel(
    table_ref, len_ref, leaf_ref, parents_ref, q_ref, tree_ref, pool_ref,
    kept_ref, m_ref, l_ref, a_ref,
):
    n_req, tree_len = parents_ref.shape
    heads = q_ref.shape[1] // HEAD_SIZE
    scale = 1.0 / math.sqrt(HEAD_SIZE)
    sub = lax.broadcasted_iota(jnp.int32, (tree_len, tree_len), 0)
    lane = lax.broadcasted_iota(jnp.int32, (tree_len, tree_len), 1)
    eye = (sub == lane).astype(jnp.float32)
    squarings = (tree_len - 1).bit_length()

    for r in range(n_req):
        rows = pl.ds(r * tree_len, tree_len)
        par = parents_ref[r : r + 1, :]
        rt = eye + (sub == par).astype(jnp.float32)
        for _ in range(squarings):
            rb = rt.astype(jnp.bfloat16)
            rt = jnp.minimum(jnp.dot(rb, rb, preferred_element_type=jnp.float32), 1.0)
        reach = nt_dot(eye.astype(jnp.bfloat16), rt.astype(jnp.bfloat16))

        depth = jnp.sum(rt, axis=0, keepdims=True) - 1.0
        leaf = leaf_ref[r]
        kept_mask = jnp.sum(jnp.where(sub == leaf, reach, 0.0), axis=0, keepdims=True)
        selector = jnp.where(
            (sub.astype(jnp.float32) == depth) & (kept_mask > 0.5), 1.0, 0.0
        ).astype(jnp.bfloat16)
        tree_rows = tree_ref[rows, :]
        kept_ref[rows, :] = jnp.dot(
            selector, tree_rows, preferred_element_type=jnp.float32
        ).astype(kept_ref.dtype)

        q_all = stacked_queries(q_ref, rows, heads)
        tree_mask = jnp.concatenate([reach] * heads, axis=0) > 0.5
        s = nt_dot(q_all, tree_rows[:, :HEAD_SIZE]) * scale
        s = jnp.where(tree_mask, s, very_negative)
        m = jnp.max(s, axis=1, keepdims=True)
        w = jnp.where(tree_mask, jnp.exp(s - m), 0.0).astype(jnp.bfloat16)
        l = jnp.sum(w.astype(jnp.float32), axis=1, keepdims=True)
        a = jnp.dot(w, tree_rows[:, HEAD_SIZE:], preferred_element_type=jnp.float32)

        pages = [pool_ref[table_ref[r, k]] for k in range(LOCAL)]
        blocks = [(m, l, a)] + page_blocks(q_all, pages, 0, len_ref[r])
        top, total, accum = merge(blocks)
        m_ref[r] = top
        l_ref[r] = total
        a_ref[r] = accum


def spill_kernel(spill_base, table_ref, len_ref, m_ref, l_ref, a_ref, q_ref, spill_ref, att_ref):
    n_req, tree_len = table_ref.shape[0], q_ref.shape[0] // table_ref.shape[0]
    heads = q_ref.shape[1] // HEAD_SIZE
    max_pages = table_ref.shape[1]
    spill_slots = spill_ref.shape[0]
    for r in range(n_req):
        rows = pl.ds(r * tree_len, tree_len)
        q_all = stacked_queries(q_ref, rows, heads)
        pages = [
            spill_ref[jnp.clip(table_ref[r, k] - spill_base, 0, spill_slots - 1)]
            for k in range(LOCAL, max_pages)
        ]
        blocks = [(m_ref[r], l_ref[r], a_ref[r])] + page_blocks(q_all, pages, LOCAL, len_ref[r])
        _, total, accum = merge(blocks)
        att = (accum / total).astype(att_ref.dtype)
        for g in range(heads):
            att_ref[rows, pl.ds(g * HEAD_SIZE, HEAD_SIZE)] = att[g * tree_len : (g + 1) * tree_len]


def shards(queries, tree_kv, page_pool, page_table, cache_len, parents, accepted, o_weight):
    requests, tree_len = parents.shape
    heads = queries.shape[1] // HEAD_SIZE
    pool_slots = page_pool[:, 0]
    own_slots = requests * LOCAL
    spill = from_behind(pool_slots[own_slots:], "req", -1)
    tree_rows = tree_kv[:, 0, :]
    smem = pl.BlockSpec(memory_space=pltpu.SMEM)
    vmem = pl.BlockSpec(memory_space=pltpu.VMEM)
    stacked = heads * tree_len
    kept, top, total, accum = pl.pallas_call(
        local_kernel,
        out_shape=(
            jax.ShapeDtypeStruct(tree_rows.shape, jnp.bfloat16),
            jax.ShapeDtypeStruct((requests, stacked, 1), jnp.float32),
            jax.ShapeDtypeStruct((requests, stacked, 1), jnp.float32),
            jax.ShapeDtypeStruct((requests, stacked, HEAD_SIZE), jnp.float32),
        ),
        in_specs=[smem, smem, smem, vmem, vmem, vmem, vmem],
        out_specs=(vmem, vmem, vmem, vmem),
    )(page_table, cache_len, accepted, parents, queries, tree_rows, pool_slots)
    attention = pl.pallas_call(
        functools.partial(spill_kernel, own_slots),
        out_shape=jax.ShapeDtypeStruct(queries.shape, jnp.bfloat16),
        in_specs=[smem, smem, vmem, vmem, vmem, vmem, vmem],
        out_specs=vmem,
    )(page_table, cache_len, top, total, accum, queries, spill)

    partial = jnp.dot(attention, o_weight, preferred_element_type=jnp.float32)
    parts = lax.axis_size("tp")
    gathered = lax.all_to_all(partial, "tp", 0, 0, tiled=True)
    blocks = gathered.reshape(parts, partial.shape[0] // parts, partial.shape[1])
    projected = jnp.sum(blocks, axis=0).astype(jnp.bfloat16)
    return (projected, kept.reshape(kept.shape[0], 1, kept.shape[1]))


def solution(mesh):
    in_specs = (
        P("req", "tp"),
        P("req", "tp", None),
        P("req", "tp", None, None),
        P("req", None),
        P("req"),
        P("req", None),
        P("req"),
        P("tp", None),
    )
    out_specs = (P(("req", "tp"), None), P("req", "tp", None))
    return jax.shard_map(shards, mesh=mesh, in_specs=in_specs, out_specs=out_specs, check_vma=False)
```

```python
import functools
import math

import jax
import jax.numpy as jnp
from jax import lax
from jax.experimental import pallas as pl
from jax.experimental.pallas import tpu as pltpu
from jax.sharding import PartitionSpec as P

HEAD_SIZE = 128
LOCAL = 2

very_negative = -1e30


def from_behind(block, axis, distance):
    devices = range(lax.axis_size(axis))
    route = [((i - distance) % len(devices), i) for i in devices]
    return lax.ppermute(block, axis, route)


def nt_dot(a, b):
    return lax.dot_general(a, b, (((1,), (1,)), ((), ())), preferred_element_type=jnp.float32)


def stacked_queries(q_ref, rows, heads):
    q = q_ref[rows, :]
    return jnp.concatenate(
        [q[:, g * HEAD_SIZE : (g + 1) * HEAD_SIZE] for g in range(heads)], axis=0
    )


def page_blocks(q_all, pages, first_page, length):
    page_len = pages[0].shape[0]
    keys = jnp.concatenate([page[:, :HEAD_SIZE] for page in pages], axis=0)
    lane = lax.broadcasted_iota(jnp.int32, (1, keys.shape[0]), 1)
    visible = (first_page * page_len + lane) < length
    scores = nt_dot(q_all, keys) * (1.0 / math.sqrt(HEAD_SIZE))
    scores = jnp.where(visible, scores, very_negative)
    blocks = []
    for k, page in enumerate(pages):
        cols = slice(k * page_len, (k + 1) * page_len)
        s = scores[:, cols]
        m = jnp.max(s, axis=1, keepdims=True)
        w = jnp.where(visible[:, cols], jnp.exp(s - m), 0.0).astype(jnp.bfloat16)
        l = jnp.sum(w.astype(jnp.float32), axis=1, keepdims=True)
        a = jnp.dot(w, page[:, HEAD_SIZE:], preferred_element_type=jnp.float32)
        blocks.append((m, l, a))
    return blocks


def merge(blocks):
    top = blocks[0][0]
    for m, _, _ in blocks[1:]:
        top = jnp.maximum(top, m)
    total = None
    accum = None
    for m, l, a in blocks:
        f = jnp.exp(m - top)
        total = f * l if total is None else total + f * l
        accum = f * a if accum is None else accum + f * a
    return top, total, accum


def local_kernel(
    table_ref, len_ref, leaf_ref, parents_ref, q_ref, tree_ref, pool_ref,
    kept_ref, m_ref, l_ref, a_ref,
):
    n_req, tree_len = parents_ref.shape
    heads = q_ref.shape[1] // HEAD_SIZE
    scale = 1.0 / math.sqrt(HEAD_SIZE)
    sub = lax.broadcasted_iota(jnp.int32, (tree_len, tree_len), 0)
    lane = lax.broadcasted_iota(jnp.int32, (tree_len, tree_len), 1)
    eye = (sub == lane).astype(jnp.float32)
    squarings = (tree_len - 1).bit_length()

    for r in range(n_req):
        rows = pl.ds(r * tree_len, tree_len)
        par = parents_ref[r : r + 1, :]
        rt = eye + (sub == par).astype(jnp.float32)
        for _ in range(squarings):
            rb = rt.astype(jnp.bfloat16)
            rt = jnp.minimum(jnp.dot(rb, rb, preferred_element_type=jnp.float32), 1.0)
        reach = nt_dot(eye.astype(jnp.bfloat16), rt.astype(jnp.bfloat16))

        depth = jnp.sum(rt, axis=0, keepdims=True) - 1.0
        leaf = leaf_ref[r]
        kept_mask = jnp.sum(jnp.where(sub == leaf, reach, 0.0), axis=0, keepdims=True)
        selector = jnp.where(
            (sub.astype(jnp.float32) == depth) & (kept_mask > 0.5), 1.0, 0.0
        ).astype(jnp.bfloat16)
        tree_rows = tree_ref[rows, :]
        kept_ref[rows, :] = jnp.dot(
            selector, tree_rows, preferred_element_type=jnp.float32
        ).astype(kept_ref.dtype)

        q_all = stacked_queries(q_ref, rows, heads)
        tree_mask = jnp.concatenate([reach] * heads, axis=0) > 0.5
        s = nt_dot(q_all, tree_rows[:, :HEAD_SIZE]) * scale
        s = jnp.where(tree_mask, s, very_negative)
        m = jnp.max(s, axis=1, keepdims=True)
        w = jnp.where(tree_mask, jnp.exp(s - m), 0.0).astype(jnp.bfloat16)
        l = jnp.sum(w.astype(jnp.float32), axis=1, keepdims=True)
        a = jnp.dot(w, tree_rows[:, HEAD_SIZE:], preferred_element_type=jnp.float32)

        pages = [pool_ref[table_ref[r, k]] for k in range(LOCAL)]
        blocks = [(m, l, a)] + page_blocks(q_all, pages, 0, len_ref[r])
        top, total, accum = merge(blocks)
        m_ref[r] = top
        l_ref[r] = total
        a_ref[r] = accum


def spill_kernel(spill_base, table_ref, len_ref, m_ref, l_ref, a_ref, q_ref, spill_ref, att_ref):
    n_req, tree_len = table_ref.shape[0], q_ref.shape[0] // table_ref.shape[0]
    heads = q_ref.shape[1] // HEAD_SIZE
    max_pages = table_ref.shape[1]
    spill_slots = spill_ref.shape[0]
    for r in range(n_req):
        rows = pl.ds(r * tree_len, tree_len)
        q_all = stacked_queries(q_ref, rows, heads)
        pages = [
            spill_ref[jnp.clip(table_ref[r, k] - spill_base, 0, spill_slots - 1)]
            for k in range(LOCAL, max_pages)
        ]
        blocks = [(m_ref[r], l_ref[r], a_ref[r])] + page_blocks(q_all, pages, LOCAL, len_ref[r])
        _, total, accum = merge(blocks)
        att = (accum / total).astype(att_ref.dtype)
        for g in range(heads):
            att_ref[rows, pl.ds(g * HEAD_SIZE, HEAD_SIZE)] = att[g * tree_len : (g + 1) * tree_len]


def shards(queries, tree_kv, page_pool, page_table, cache_len, parents, accepted, o_weight):
    requests, tree_len = parents.shape
    heads = queries.shape[1] // HEAD_SIZE
    pool_slots = page_pool[:, 0]
    own_slots = requests * LOCAL
    spill = from_behind(pool_slots[own_slots:], "req", -1)
    tree_rows = tree_kv[:, 0, :]
    smem = pl.BlockSpec(memory_space=pltpu.SMEM)
    vmem = pl.BlockSpec(memory_space=pltpu.VMEM)
    stacked = heads * tree_len
    kept, top, total, accum = pl.pallas_call(
        local_kernel,
        out_shape=(
            jax.ShapeDtypeStruct(tree_rows.shape, jnp.bfloat16),
            jax.ShapeDtypeStruct((requests, stacked, 1), jnp.float32),
            jax.ShapeDtypeStruct((requests, stacked, 1), jnp.float32),
            jax.ShapeDtypeStruct((requests, stacked, HEAD_SIZE), jnp.float32),
        ),
        in_specs=[smem, smem, smem, vmem, vmem, vmem, vmem],
        out_specs=(vmem, vmem, vmem, vmem),
    )(page_table, cache_len, accepted, parents, queries, tree_rows, pool_slots)
    attention = pl.pallas_call(
        functools.partial(spill_kernel, own_slots),
        out_shape=jax.ShapeDtypeStruct(queries.shape, jnp.bfloat16),
        in_specs=[smem, smem, vmem, vmem, vmem, vmem, vmem],
        out_specs=vmem,
    )(page_table, cache_len, top, total, accum, queries, spill)

    partial = jnp.dot(attention, o_weight, preferred_element_type=jnp.float32)
    parts = lax.axis_size("tp")
    gathered = lax.all_to_all(partial.astype(jnp.bfloat16), "tp", 0, 0, tiled=True)
    blocks = gathered.reshape(parts, partial.shape[0] // parts, partial.shape[1])
    summed = blocks[0].astype(jnp.float32)
    for i in range(1, parts):
        summed = summed + blocks[i].astype(jnp.float32)
    projected = summed.astype(jnp.bfloat16)
    return (projected, kept.reshape(kept.shape[0], 1, kept.shape[1]))


def solution(mesh):
    in_specs = (
        P("req", "tp"),
        P("req", "tp", None),
        P("req", "tp", None, None),
        P("req", None),
        P("req"),
        P("req", None),
        P("req"),
        P("tp", None),
    )
    out_specs = (P(("req", "tp"), None), P("req", "tp", None))
    return jax.shard_map(shards, mesh=mesh, in_specs=in_specs, out_specs=out_specs, check_vma=False)
```

```python
import functools
import math

import jax
import jax.numpy as jnp
from jax import lax
from jax.experimental import pallas as pl
from jax.experimental.pallas import tpu as pltpu
from jax.sharding import PartitionSpec as P

HEAD_SIZE = 128
LOCAL = 2

very_negative = -1e30


def from_behind(block, axis, distance):
    devices = range(lax.axis_size(axis))
    route = [((i - distance) % len(devices), i) for i in devices]
    return lax.ppermute(block, axis, route)


def nt_dot(a, b):
    return lax.dot_general(a, b, (((1,), (1,)), ((), ())), preferred_element_type=jnp.float32)


def stacked_queries(q_ref, rows, heads):
    q = q_ref[rows, :]
    return jnp.concatenate(
        [q[:, g * HEAD_SIZE : (g + 1) * HEAD_SIZE] for g in range(heads)], axis=0
    )


def page_blocks(q_all, pages, first_page, length):
    page_len = pages[0].shape[0]
    keys = jnp.concatenate([page[:, :HEAD_SIZE] for page in pages], axis=0)
    lane = lax.broadcasted_iota(jnp.int32, (1, keys.shape[0]), 1)
    visible = (first_page * page_len + lane) < length
    scores = nt_dot(q_all, keys) * (1.0 / math.sqrt(HEAD_SIZE))
    scores = jnp.where(visible, scores, very_negative)
    blocks = []
    for k, page in enumerate(pages):
        cols = slice(k * page_len, (k + 1) * page_len)
        s = scores[:, cols]
        m = jnp.max(s, axis=1, keepdims=True)
        w = jnp.where(visible[:, cols], jnp.exp(s - m), 0.0).astype(jnp.bfloat16)
        l = jnp.sum(w.astype(jnp.float32), axis=1, keepdims=True)
        a = jnp.dot(w, page[:, HEAD_SIZE:], preferred_element_type=jnp.float32)
        blocks.append((m, l, a))
    return blocks


def merge(blocks):
    top = blocks[0][0]
    for m, _, _ in blocks[1:]:
        top = jnp.maximum(top, m)
    total = None
    accum = None
    for m, l, a in blocks:
        f = jnp.exp(m - top)
        total = f * l if total is None else total + f * l
        accum = f * a if accum is None else accum + f * a
    return top, total, accum


def local_kernel(
    table_ref, len_ref, leaf_ref, parents_ref, q_ref, tree_ref, pool_ref,
    kept_ref, ml_ref, a_ref,
):
    nodes = parents_ref.shape[1]
    n_req = table_ref.shape[0]
    tree_len = nodes // n_req
    heads = q_ref.shape[1] // HEAD_SIZE
    stacked = heads * tree_len
    scale = 1.0 / math.sqrt(HEAD_SIZE)
    sub = lax.broadcasted_iota(jnp.int32, (nodes, nodes), 0)
    lane = lax.broadcasted_iota(jnp.int32, (nodes, nodes), 1)
    eye = (sub == lane).astype(jnp.float32)
    squarings = (tree_len - 1).bit_length()

    rt = eye + (sub == parents_ref[...]).astype(jnp.float32)
    for _ in range(squarings):
        rb = rt.astype(jnp.bfloat16)
        rt = jnp.minimum(jnp.dot(rb, rb, preferred_element_type=jnp.float32), 1.0)
    reach = nt_dot(eye.astype(jnp.bfloat16), rt.astype(jnp.bfloat16))

    depth = jnp.sum(rt, axis=0, keepdims=True) - 1.0
    slot = lax.broadcasted_iota(jnp.int32, (tree_len, nodes), 0).astype(jnp.float32)
    selectors = []
    for r in range(n_req):
        leaf = r * tree_len + leaf_ref[r]
        kept_mask = jnp.sum(jnp.where(sub == leaf, reach, 0.0), axis=0, keepdims=True)
        selectors.append(jnp.where((slot == depth) & (kept_mask > 0.5), 1.0, 0.0))
    selector = jnp.concatenate(selectors, axis=0).astype(jnp.bfloat16)
    tree_rows = tree_ref[...]
    kept_ref[...] = jnp.dot(selector, tree_rows, preferred_element_type=jnp.float32).astype(
        kept_ref.dtype
    )

    q_all = [stacked_queries(q_ref, pl.ds(r * tree_len, tree_len), heads) for r in range(n_req)]
    tree_mask = (
        jnp.concatenate(
            [reach[r * tree_len : (r + 1) * tree_len] for r in range(n_req) for _ in range(heads)],
            axis=0,
        )
        > 0.5
    )
    s = nt_dot(jnp.concatenate(q_all, axis=0), tree_rows[:, :HEAD_SIZE]) * scale
    s = jnp.where(tree_mask, s, very_negative)
    m = jnp.max(s, axis=1, keepdims=True)
    w = jnp.where(tree_mask, jnp.exp(s - m), 0.0).astype(jnp.bfloat16)
    l = jnp.sum(w.astype(jnp.float32), axis=1, keepdims=True)
    a = jnp.dot(w, tree_rows[:, HEAD_SIZE:], preferred_element_type=jnp.float32)

    state_lane = lax.broadcasted_iota(jnp.int32, (stacked, HEAD_SIZE), 1)
    for r in range(n_req):
        rows = slice(r * stacked, (r + 1) * stacked)
        pages = [pool_ref[table_ref[r, k]] for k in range(LOCAL)]
        blocks = [(m[rows], l[rows], a[rows])] + page_blocks(q_all[r], pages, 0, len_ref[r])
        top, total, accum = merge(blocks)
        ml_ref[r] = jnp.where(state_lane == 0, top, jnp.where(state_lane == 1, total, 0.0))
        a_ref[r] = accum


def spill_kernel(spill_base, table_ref, len_ref, ml_ref, a_ref, q_ref, spill_ref, att_ref):
    n_req, tree_len = table_ref.shape[0], q_ref.shape[0] // table_ref.shape[0]
    heads = q_ref.shape[1] // HEAD_SIZE
    max_pages = table_ref.shape[1]
    spill_slots = spill_ref.shape[0]
    page_len = spill_ref.shape[1]
    for r in range(n_req):
        rows = pl.ds(r * tree_len, tree_len)
        length = len_ref[r]

        def write(att):
            for g in range(heads):
                att_ref[rows, pl.ds(g * HEAD_SIZE, HEAD_SIZE)] = att[g * tree_len : (g + 1) * tree_len]

        @pl.when(length > LOCAL * page_len)
        def _():
            q_all = stacked_queries(q_ref, rows, heads)
            pages = [
                spill_ref[jnp.clip(table_ref[r, k] - spill_base, 0, spill_slots - 1)]
                for k in range(LOCAL, max_pages)
            ]
            ml = ml_ref[r]
            state = (ml[:, 0:1], ml[:, 1:2], a_ref[r])
            _, total, accum = merge([state] + page_blocks(q_all, pages, LOCAL, length))
            write((accum / total).astype(att_ref.dtype))

        @pl.when(length <= LOCAL * page_len)
        def _():
            ml = ml_ref[r]
            write((a_ref[r] / ml[:, 1:2]).astype(att_ref.dtype))


def shards(queries, tree_kv, page_pool, page_table, cache_len, parents, accepted, o_weight):
    requests, tree_len = parents.shape
    heads = queries.shape[1] // HEAD_SIZE
    pool_slots = page_pool[:, 0]
    own_slots = requests * LOCAL
    spill = from_behind(pool_slots[own_slots:], "req", -1)
    tree_rows = tree_kv[:, 0, :]
    smem = pl.BlockSpec(memory_space=pltpu.SMEM)
    vmem = pl.BlockSpec(memory_space=pltpu.VMEM)
    stacked = heads * tree_len
    offsets = (jnp.arange(requests, dtype=jnp.int32) * tree_len)[:, None]
    parent_ids = jnp.where(parents >= 0, parents + offsets, -1).reshape(1, requests * tree_len)
    kept, packed, accum = pl.pallas_call(
        local_kernel,
        out_shape=(
            jax.ShapeDtypeStruct(tree_rows.shape, jnp.bfloat16),
            jax.ShapeDtypeStruct((requests, stacked, HEAD_SIZE), jnp.float32),
            jax.ShapeDtypeStruct((requests, stacked, HEAD_SIZE), jnp.float32),
        ),
        in_specs=[smem, smem, smem, vmem, vmem, vmem, vmem],
        out_specs=(vmem, vmem, vmem),
    )(page_table, cache_len, accepted, parent_ids, queries, tree_rows, pool_slots)
    attention = pl.pallas_call(
        functools.partial(spill_kernel, own_slots),
        out_shape=jax.ShapeDtypeStruct(queries.shape, jnp.bfloat16),
        in_specs=[smem, smem, vmem, vmem, vmem, vmem],
        out_specs=vmem,
    )(page_table, cache_len, packed, accum, queries, spill)

    partial = jnp.dot(attention, o_weight, preferred_element_type=jnp.float32)
    parts = lax.axis_size("tp")
    gathered = lax.all_to_all(partial.astype(jnp.bfloat16), "tp", 0, 0, tiled=True)
    blocks = gathered.reshape(parts, partial.shape[0] // parts, partial.shape[1])
    summed = blocks[0].astype(jnp.float32)
    for i in range(1, parts):
        summed = summed + blocks[i].astype(jnp.float32)
    projected = summed.astype(jnp.bfloat16)
    return (projected, kept.reshape(kept.shape[0], 1, kept.shape[1]))


def solution(mesh):
    in_specs = (
        P("req", "tp"),
        P("req", "tp", None),
        P("req", "tp", None, None),
        P("req", None),
        P("req"),
        P("req", None),
        P("req"),
        P("tp", None),
    )
    out_specs = (P(("req", "tp"), None), P("req", "tp", None))
    return jax.shard_map(shards, mesh=mesh, in_specs=in_specs, out_specs=out_specs, check_vma=False)
```

```python
import functools
import math

import jax
import jax.numpy as jnp
from jax import lax
from jax.experimental import pallas as pl
from jax.experimental.pallas import tpu as pltpu
from jax.sharding import PartitionSpec as P


HEAD_SIZE = 128
LOCAL = 2

very_negative = -1e30


def nt_dot(a, b):
    return lax.dot_general(a, b, (((1,), (1,)), ((), ())), preferred_element_type=jnp.float32)


def stacked_queries(q_ref, rows, heads):
    q = q_ref[rows, :]
    return jnp.concatenate(
        [q[:, g * HEAD_SIZE : (g + 1) * HEAD_SIZE] for g in range(heads)], axis=0
    )


def page_blocks(q_all, pages, first_page, length):
    page_len = pages[0].shape[0]
    keys = jnp.concatenate([page[:, :HEAD_SIZE] for page in pages], axis=0)
    lane = lax.broadcasted_iota(jnp.int32, (1, keys.shape[0]), 1)
    visible = (first_page * page_len + lane) < length
    scores = nt_dot(q_all, keys) * (1.0 / math.sqrt(HEAD_SIZE))
    scores = jnp.where(visible, scores, very_negative)
    blocks = []
    for k, page in enumerate(pages):
        cols = slice(k * page_len, (k + 1) * page_len)
        s = scores[:, cols]
        m = jnp.max(s, axis=1, keepdims=True)
        w = jnp.where(visible[:, cols], jnp.exp(s - m), 0.0).astype(jnp.bfloat16)
        l = jnp.sum(w.astype(jnp.float32), axis=1, keepdims=True)
        a = jnp.dot(w, page[:, HEAD_SIZE:], preferred_element_type=jnp.float32)
        blocks.append((m, l, a))
    return blocks


def merge(blocks):
    top = blocks[0][0]
    for m, _, _ in blocks[1:]:
        top = jnp.maximum(top, m)
    total = None
    accum = None
    for m, l, a in blocks:
        f = jnp.exp(m - top)
        total = f * l if total is None else total + f * l
        accum = f * a if accum is None else accum + f * a
    return top, total, accum


def local_kernel(
    table_ref, len_ref, leaf_ref, parents_ref, q_ref, tree_ref, pool_ref,
    kept_ref, ml_ref, a_ref,
):
    n_req, tree_len = parents_ref.shape
    nodes = n_req * tree_len
    heads = q_ref.shape[1] // HEAD_SIZE
    stacked = heads * tree_len
    scale = 1.0 / math.sqrt(HEAD_SIZE)
    sub = lax.broadcasted_iota(jnp.int32, (nodes, nodes), 0)
    lane = lax.broadcasted_iota(jnp.int32, (nodes, nodes), 1)
    eye = (sub == lane).astype(jnp.float32)
    squarings = (tree_len - 1).bit_length()

    parents = parents_ref[...].astype(jnp.float32)
    first = lax.broadcasted_iota(jnp.int32, parents.shape, 0).astype(jnp.float32) * tree_len
    parents = jnp.where(parents >= 0.0, parents + first, -1.0).astype(jnp.bfloat16)
    node = lax.broadcasted_iota(jnp.int32, (tree_len, nodes), 0)
    column = lax.broadcasted_iota(jnp.int32, (tree_len, nodes), 1)
    parent_row = None
    for r in range(n_req):
        place = (column == node + r * tree_len).astype(jnp.bfloat16)
        lhs = jnp.broadcast_to(parents[r : r + 1], (16, tree_len))
        placed = jnp.dot(lhs, place, preferred_element_type=jnp.float32)[0:1]
        parent_row = placed if parent_row is None else parent_row + placed

    rt = eye + (sub.astype(jnp.float32) == parent_row).astype(jnp.float32)
    for _ in range(squarings):
        rb = rt.astype(jnp.bfloat16)
        rt = jnp.minimum(jnp.dot(rb, rb, preferred_element_type=jnp.float32), 1.0)
    reach = nt_dot(eye.astype(jnp.bfloat16), rt.astype(jnp.bfloat16))

    depth = jnp.sum(rt, axis=0, keepdims=True) - 1.0
    slot = lax.broadcasted_iota(jnp.int32, (tree_len, nodes), 0).astype(jnp.float32)
    selectors = []
    for r in range(n_req):
        leaf = r * tree_len + leaf_ref[r]
        kept_mask = jnp.sum(jnp.where(sub == leaf, reach, 0.0), axis=0, keepdims=True)
        selectors.append(jnp.where((slot == depth) & (kept_mask > 0.5), 1.0, 0.0))
    selector = jnp.concatenate(selectors, axis=0).astype(jnp.bfloat16)
    tree_rows = tree_ref[...]
    kept_ref[...] = jnp.dot(selector, tree_rows, preferred_element_type=jnp.float32).astype(
        kept_ref.dtype
    )

    q_all = [stacked_queries(q_ref, pl.ds(r * tree_len, tree_len), heads) for r in range(n_req)]
    tree_mask = (
        jnp.concatenate(
            [reach[r * tree_len : (r + 1) * tree_len] for r in range(n_req) for _ in range(heads)],
            axis=0,
        )
        > 0.5
    )
    s = nt_dot(jnp.concatenate(q_all, axis=0), tree_rows[:, :HEAD_SIZE]) * scale
    s = jnp.where(tree_mask, s, very_negative)
    m = jnp.max(s, axis=1, keepdims=True)
    w = jnp.where(tree_mask, jnp.exp(s - m), 0.0).astype(jnp.bfloat16)
    l = jnp.sum(w.astype(jnp.float32), axis=1, keepdims=True)
    a = jnp.dot(w, tree_rows[:, HEAD_SIZE:], preferred_element_type=jnp.float32)

    state_lane = lax.broadcasted_iota(jnp.int32, (stacked, HEAD_SIZE), 1)
    for r in range(n_req):
        rows = slice(r * stacked, (r + 1) * stacked)
        pages = [pool_ref[table_ref[r, k]] for k in range(LOCAL)]
        blocks = [(m[rows], l[rows], a[rows])] + page_blocks(q_all[r], pages, 0, len_ref[r])
        top, total, accum = merge(blocks)
        ml_ref[r] = jnp.where(state_lane == 0, top, jnp.where(state_lane == 1, total, 0.0))
        a_ref[r] = accum


def spill_kernel(
    spill_base, table_ref, len_ref, flag_ref, ml_ref, a_ref, q_ref, spill_ref, far_ref, att_ref
):
    n_req, tree_len = table_ref.shape[0], q_ref.shape[0] // table_ref.shape[0]
    heads = q_ref.shape[1] // HEAD_SIZE
    max_pages = table_ref.shape[1]
    spill_slots = spill_ref.shape[0]
    page_len = spill_ref.shape[1]
    for r in range(n_req):
        rows = pl.ds(r * tree_len, tree_len)
        length = len_ref[r]

        def write(att):
            for g in range(heads):
                att_ref[rows, pl.ds(g * HEAD_SIZE, HEAD_SIZE)] = att[g * tree_len : (g + 1) * tree_len]

        @pl.when(length > LOCAL * page_len)
        def _():
            q_all = stacked_queries(q_ref, rows, heads)
            far = flag_ref[0] > 0
            pages = []
            for k in range(LOCAL, max_pages):
                index = jnp.clip(table_ref[r, k] - spill_base, 0, spill_slots - 1)
                pages.append(jnp.where(far, far_ref[index], spill_ref[index]))
            ml = ml_ref[r]
            state = (ml[:, 0:1], ml[:, 1:2], a_ref[r])
            _, total, accum = merge([state] + page_blocks(q_all, pages, LOCAL, length))
            write((accum / total).astype(att_ref.dtype))

        @pl.when(length <= LOCAL * page_len)
        def _():
            ml = ml_ref[r]
            write((a_ref[r] / ml[:, 1:2]).astype(att_ref.dtype))


def step(queries, tree_kv, page_pool, page_table, cache_len, parents, accepted, o_weight):
    requests, tree_len = parents.shape
    heads = queries.shape[1] // HEAD_SIZE
    pool_slots = page_pool[:, 0]
    own_slots = requests * LOCAL
    ring = lax.axis_size("req")
    spill_source = pool_slots[own_slots:]
    spill = lax.ppermute(spill_source, "req", [(i + 1, i) for i in range(ring - 1)])
    tree_rows = tree_kv[:, 0, :]
    smem = pl.BlockSpec(memory_space=pltpu.SMEM)
    vmem = pl.BlockSpec(memory_space=pltpu.VMEM)
    stacked = heads * tree_len
    local_call = pl.pallas_call(
        local_kernel,
        out_shape=(
            jax.ShapeDtypeStruct(tree_rows.shape, jnp.bfloat16),
            jax.ShapeDtypeStruct((requests, stacked, HEAD_SIZE), jnp.float32),
            jax.ShapeDtypeStruct((requests, stacked, HEAD_SIZE), jnp.float32),
        ),
        in_specs=[smem, smem, smem, vmem, vmem, vmem, vmem],
        out_specs=(vmem, vmem, vmem),
    )
    kept, packed, accum = local_call(
        page_table, cache_len, accepted, parents, queries, tree_rows, pool_slots
    )
    kept, packed, accum, spill_source = lax.optimization_barrier((kept, packed, accum, spill_source))
    far_spill = lax.ppermute(spill_source, "req", [(0, ring - 1)])
    far_flag = (lax.axis_index("req") == ring - 1).astype(jnp.int32).reshape(1)
    attention = pl.pallas_call(
        functools.partial(spill_kernel, own_slots),
        out_shape=jax.ShapeDtypeStruct(queries.shape, jnp.bfloat16),
        in_specs=[smem, smem, smem, vmem, vmem, vmem, vmem, vmem],
        out_specs=vmem,
    )(page_table, cache_len, far_flag, packed, accum, queries, spill, far_spill)

    partial = jnp.dot(attention, o_weight, preferred_element_type=jnp.float32)
    parts = lax.axis_size("tp")
    gathered = lax.all_to_all(partial.astype(jnp.bfloat16), "tp", 0, 0, tiled=True)
    blocks = gathered.reshape(parts, partial.shape[0] // parts, partial.shape[1])
    summed = blocks[0].astype(jnp.float32)
    for i in range(1, parts):
        summed = summed + blocks[i].astype(jnp.float32)
    projected = summed.astype(jnp.bfloat16)
    return (projected, kept.reshape(kept.shape[0], 1, kept.shape[1]))


def solution(mesh):
    in_specs = (
        P("req", "tp"),
        P("req", "tp", None),
        P("req", "tp", None, None),
        P("req", None),
        P("req"),
        P("req", None),
        P("req"),
        P("tp", None),
    )
    out_specs = (P(("req", "tp"), None), P("req", "tp", None))
    return jax.shard_map(step, mesh=mesh, in_specs=in_specs, out_specs=out_specs, check_vma=False)
```

```python
import functools
import math

import jax
import jax.numpy as jnp
from jax import lax
from jax.experimental import pallas as pl
from jax.experimental.pallas import tpu as pltpu
from jax.sharding import PartitionSpec as P

HEAD_SIZE = 128
LOCAL = 2

very_negative = -1e30


def nt_dot(a, b):
    return lax.dot_general(a, b, (((1,), (1,)), ((), ())), preferred_element_type=jnp.float32)


def stacked_queries(q_ref, rows, heads):
    q = q_ref[rows, :]
    return jnp.concatenate(
        [q[:, g * HEAD_SIZE : (g + 1) * HEAD_SIZE] for g in range(heads)], axis=0
    )


def page_blocks(q_all, pages, first_page, length):
    page_len = pages[0].shape[0]
    keys = jnp.concatenate([page[:, :HEAD_SIZE] for page in pages], axis=0)
    lane = lax.broadcasted_iota(jnp.int32, (1, keys.shape[0]), 1)
    visible = (first_page * page_len + lane) < length
    scores = nt_dot(q_all, keys) * (1.0 / math.sqrt(HEAD_SIZE))
    scores = jnp.where(visible, scores, very_negative)
    blocks = []
    for k, page in enumerate(pages):
        cols = slice(k * page_len, (k + 1) * page_len)
        s = scores[:, cols]
        m = jnp.max(s, axis=1, keepdims=True)
        w = jnp.where(visible[:, cols], jnp.exp(s - m), 0.0).astype(jnp.bfloat16)
        l = jnp.sum(w.astype(jnp.float32), axis=1, keepdims=True)
        a = jnp.dot(w, page[:, HEAD_SIZE:], preferred_element_type=jnp.float32)
        blocks.append((m, l, a))
    return blocks


def merge(blocks):
    top = blocks[0][0]
    for m, _, _ in blocks[1:]:
        top = jnp.maximum(top, m)
    total = None
    accum = None
    for m, l, a in blocks:
        f = jnp.exp(m - top)
        total = f * l if total is None else total + f * l
        accum = f * a if accum is None else accum + f * a
    return top, total, accum


def local_kernel(
    table_ref, len_ref, leaf_ref, parents_ref, q_ref, tree_ref, pool_ref,
    kept_ref, ml_ref, a_ref,
):
    n_req, tree_len = parents_ref.shape
    nodes = n_req * tree_len
    heads = q_ref.shape[1] // HEAD_SIZE
    stacked = heads * tree_len
    scale = 1.0 / math.sqrt(HEAD_SIZE)
    sub = lax.broadcasted_iota(jnp.int32, (nodes, nodes), 0)
    lane = lax.broadcasted_iota(jnp.int32, (nodes, nodes), 1)
    eye = (sub == lane).astype(jnp.float32)
    squarings = (tree_len - 1).bit_length()

    parents = parents_ref[...].astype(jnp.float32)
    first = lax.broadcasted_iota(jnp.int32, parents.shape, 0).astype(jnp.float32) * tree_len
    parents = jnp.where(parents >= 0.0, parents + first, -1.0).astype(jnp.bfloat16)
    node = lax.broadcasted_iota(jnp.int32, (tree_len, nodes), 0)
    column = lax.broadcasted_iota(jnp.int32, (tree_len, nodes), 1)
    parent_row = None
    for r in range(n_req):
        place = (column == node + r * tree_len).astype(jnp.bfloat16)
        lhs = jnp.broadcast_to(parents[r : r + 1], (16, tree_len))
        placed = jnp.dot(lhs, place, preferred_element_type=jnp.float32)[0:1]
        parent_row = placed if parent_row is None else parent_row + placed

    rt = eye + (sub.astype(jnp.float32) == parent_row).astype(jnp.float32)
    for _ in range(squarings):
        rb = rt.astype(jnp.bfloat16)
        rt = jnp.minimum(jnp.dot(rb, rb, preferred_element_type=jnp.float32), 1.0)
    reach = nt_dot(eye.astype(jnp.bfloat16), rt.astype(jnp.bfloat16))

    depth = jnp.sum(rt, axis=0, keepdims=True) - 1.0
    slot = lax.broadcasted_iota(jnp.int32, (tree_len, nodes), 0).astype(jnp.float32)
    selectors = []
    for r in range(n_req):
        leaf = r * tree_len + leaf_ref[r]
        kept_mask = jnp.sum(jnp.where(sub == leaf, reach, 0.0), axis=0, keepdims=True)
        selectors.append(jnp.where((slot == depth) & (kept_mask > 0.5), 1.0, 0.0))
    selector = jnp.concatenate(selectors, axis=0).astype(jnp.bfloat16)
    tree_rows = tree_ref[...]
    kept_ref[...] = jnp.dot(selector, tree_rows, preferred_element_type=jnp.float32).astype(
        kept_ref.dtype
    )

    q_all = [stacked_queries(q_ref, pl.ds(r * tree_len, tree_len), heads) for r in range(n_req)]
    tree_mask = (
        jnp.concatenate(
            [reach[r * tree_len : (r + 1) * tree_len] for r in range(n_req) for _ in range(heads)],
            axis=0,
        )
        > 0.5
    )
    s = nt_dot(jnp.concatenate(q_all, axis=0), tree_rows[:, :HEAD_SIZE]) * scale
    s = jnp.where(tree_mask, s, very_negative)
    m = jnp.max(s, axis=1, keepdims=True)
    w = jnp.where(tree_mask, jnp.exp(s - m), 0.0).astype(jnp.bfloat16)
    l = jnp.sum(w.astype(jnp.float32), axis=1, keepdims=True)
    a = jnp.dot(w, tree_rows[:, HEAD_SIZE:], preferred_element_type=jnp.float32)

    state_lane = lax.broadcasted_iota(jnp.int32, (stacked, HEAD_SIZE), 1)
    for r in range(n_req):
        rows = slice(r * stacked, (r + 1) * stacked)
        pages = [pool_ref[table_ref[r, k]] for k in range(LOCAL)]
        blocks = [(m[rows], l[rows], a[rows])] + page_blocks(q_all[r], pages, 0, len_ref[r])
        top, total, accum = merge(blocks)
        ml_ref[r] = jnp.where(state_lane == 0, top, jnp.where(state_lane == 1, total, 0.0))
        a_ref[r] = accum


def spill_kernel(spill_base, table_ref, len_ref, ml_ref, a_ref, q_ref, spill_ref, att_ref):
    n_req, tree_len = table_ref.shape[0], q_ref.shape[0] // table_ref.shape[0]
    heads = q_ref.shape[1] // HEAD_SIZE
    max_pages = table_ref.shape[1]
    spill_slots = spill_ref.shape[0]
    page_len = spill_ref.shape[1]
    for r in range(n_req):
        rows = pl.ds(r * tree_len, tree_len)
        length = len_ref[r]

        def write(att):
            for g in range(heads):
                att_ref[rows, pl.ds(g * HEAD_SIZE, HEAD_SIZE)] = att[g * tree_len : (g + 1) * tree_len]

        @pl.when(length > LOCAL * page_len)
        def _():
            q_all = stacked_queries(q_ref, rows, heads)
            pages = [
                spill_ref[jnp.clip(table_ref[r, k] - spill_base, 0, spill_slots - 1)]
                for k in range(LOCAL, max_pages)
            ]
            ml = ml_ref[r]
            state = (ml[:, 0:1], ml[:, 1:2], a_ref[r])
            _, total, accum = merge([state] + page_blocks(q_all, pages, LOCAL, length))
            write((accum / total).astype(att_ref.dtype))

        @pl.when(length <= LOCAL * page_len)
        def _():
            ml = ml_ref[r]
            write((a_ref[r] / ml[:, 1:2]).astype(att_ref.dtype))


def step(queries, tree_kv, page_pool, page_table, cache_len, parents, accepted, o_weight):
    requests, tree_len = parents.shape
    heads = queries.shape[1] // HEAD_SIZE
    pool_slots = page_pool[:, 0]
    own_slots = requests * LOCAL
    ring = lax.axis_size("req")
    spill_source = pool_slots[own_slots:]
    spill = lax.ppermute(spill_source, "req", [((i + 1) % ring, i) for i in range(ring)])
    tree_rows = tree_kv[:, 0, :]
    smem = pl.BlockSpec(memory_space=pltpu.SMEM)
    vmem = pl.BlockSpec(memory_space=pltpu.VMEM)
    stacked = heads * tree_len
    local_call = pl.pallas_call(
        local_kernel,
        out_shape=(
            jax.ShapeDtypeStruct(tree_rows.shape, jnp.bfloat16),
            jax.ShapeDtypeStruct((requests, stacked, HEAD_SIZE), jnp.float32),
            jax.ShapeDtypeStruct((requests, stacked, HEAD_SIZE), jnp.float32),
        ),
        in_specs=[smem, smem, smem, vmem, vmem, vmem, vmem],
        out_specs=(vmem, vmem, vmem),
    )
    kept, packed, accum = local_call(
        page_table, cache_len, accepted, parents, queries, tree_rows, pool_slots
    )
    attention = pl.pallas_call(
        functools.partial(spill_kernel, own_slots),
        out_shape=jax.ShapeDtypeStruct(queries.shape, jnp.bfloat16),
        in_specs=[smem, smem, vmem, vmem, vmem, vmem],
        out_specs=vmem,
    )(page_table, cache_len, packed, accum, queries, spill)

    partial = jnp.dot(attention, o_weight, preferred_element_type=jnp.float32)
    parts = lax.axis_size("tp")
    gathered = lax.all_to_all(partial.astype(jnp.bfloat16), "tp", 0, 0, tiled=True)
    blocks = gathered.reshape(parts, partial.shape[0] // parts, partial.shape[1])
    summed = blocks[0].astype(jnp.float32)
    for i in range(1, parts):
        summed = summed + blocks[i].astype(jnp.float32)
    projected = summed.astype(jnp.bfloat16)
    return (projected, kept.reshape(kept.shape[0], 1, kept.shape[1]))


def solution(mesh):
    in_specs = (
        P("req", "tp"),
        P("req", "tp", None),
        P("req", "tp", None, None),
        P("req", None),
        P("req"),
        P("req", None),
        P("req"),
        P("tp", None),
    )
    out_specs = (P(("req", "tp"), None), P("req", "tp", None))
    return jax.shard_map(step, mesh=mesh, in_specs=in_specs, out_specs=out_specs, check_vma=False)
```

```python
import functools
import math

import jax
import jax.numpy as jnp
from jax import lax
from jax.experimental import pallas as pl
from jax.experimental.pallas import tpu as pltpu
from jax.sharding import PartitionSpec as P

HEAD_SIZE = 128
LOCAL = 2

very_negative = -1e30


def nt_dot(a, b):
    return lax.dot_general(a, b, (((1,), (1,)), ((), ())), preferred_element_type=jnp.float32)


def stacked_queries(q_ref, rows, heads):
    q = q_ref[rows, :]
    return jnp.concatenate(
        [q[:, g * HEAD_SIZE : (g + 1) * HEAD_SIZE] for g in range(heads)], axis=0
    )


def page_blocks(q_all, pages, first_page, length):
    page_len = pages[0].shape[0]
    keys = jnp.concatenate([page[:, :HEAD_SIZE] for page in pages], axis=0)
    lane = lax.broadcasted_iota(jnp.int32, (1, keys.shape[0]), 1)
    visible = (first_page * page_len + lane) < length
    scores = nt_dot(q_all, keys) * (1.0 / math.sqrt(HEAD_SIZE))
    scores = jnp.where(visible, scores, very_negative)
    blocks = []
    for k, page in enumerate(pages):
        cols = slice(k * page_len, (k + 1) * page_len)
        s = scores[:, cols]
        m = jnp.max(s, axis=1, keepdims=True)
        w = jnp.where(visible[:, cols], jnp.exp(s - m), 0.0).astype(jnp.bfloat16)
        l = jnp.sum(w.astype(jnp.float32), axis=1, keepdims=True)
        a = jnp.dot(w, page[:, HEAD_SIZE:], preferred_element_type=jnp.float32)
        blocks.append((m, l, a))
    return blocks


def merge(blocks):
    top = blocks[0][0]
    for m, _, _ in blocks[1:]:
        top = jnp.maximum(top, m)
    total = None
    accum = None
    for m, l, a in blocks:
        f = jnp.exp(m - top)
        total = f * l if total is None else total + f * l
        accum = f * a if accum is None else accum + f * a
    return top, total, accum


def merged_kernel(
    spill_base, table_ref, len_ref, leaf_ref, parents_ref, q_ref, tree_ref, pool_ref, spill_ref,
    weight_hbm, proj_ref, kept_ref, weight_vmem, att_sc, weight_sem,
):
    weight_copy = pltpu.make_async_copy(weight_hbm, weight_vmem, weight_sem)
    weight_copy.start()

    n_req, tree_len = parents_ref.shape
    nodes = n_req * tree_len
    heads = q_ref.shape[1] // HEAD_SIZE
    stacked = heads * tree_len
    max_pages = table_ref.shape[1]
    spill_slots = spill_ref.shape[0]
    scale = 1.0 / math.sqrt(HEAD_SIZE)
    sub = lax.broadcasted_iota(jnp.int32, (nodes, nodes), 0)
    lane = lax.broadcasted_iota(jnp.int32, (nodes, nodes), 1)
    eye = (sub == lane).astype(jnp.float32)
    squarings = (tree_len - 1).bit_length()

    parents = parents_ref[...].astype(jnp.float32)
    first = lax.broadcasted_iota(jnp.int32, parents.shape, 0).astype(jnp.float32) * tree_len
    parents = jnp.where(parents >= 0.0, parents + first, -1.0).astype(jnp.bfloat16)
    node = lax.broadcasted_iota(jnp.int32, (tree_len, nodes), 0)
    column = lax.broadcasted_iota(jnp.int32, (tree_len, nodes), 1)
    parent_row = None
    for r in range(n_req):
        place = (column == node + r * tree_len).astype(jnp.bfloat16)
        lhs = jnp.broadcast_to(parents[r : r + 1], (16, tree_len))
        placed = jnp.dot(lhs, place, preferred_element_type=jnp.float32)[0:1]
        parent_row = placed if parent_row is None else parent_row + placed

    rt = eye + (sub.astype(jnp.float32) == parent_row).astype(jnp.float32)
    for _ in range(squarings):
        rb = rt.astype(jnp.bfloat16)
        rt = jnp.minimum(jnp.dot(rb, rb, preferred_element_type=jnp.float32), 1.0)
    reach = nt_dot(eye.astype(jnp.bfloat16), rt.astype(jnp.bfloat16))

    depth = jnp.sum(rt, axis=0, keepdims=True) - 1.0
    slot = lax.broadcasted_iota(jnp.int32, (tree_len, nodes), 0).astype(jnp.float32)
    selectors = []
    for r in range(n_req):
        leaf = r * tree_len + leaf_ref[r]
        kept_mask = jnp.sum(jnp.where(sub == leaf, reach, 0.0), axis=0, keepdims=True)
        selectors.append(jnp.where((slot == depth) & (kept_mask > 0.5), 1.0, 0.0))
    selector = jnp.concatenate(selectors, axis=0).astype(jnp.bfloat16)
    tree_rows = tree_ref[...]
    kept_ref[...] = jnp.dot(selector, tree_rows, preferred_element_type=jnp.float32).astype(
        kept_ref.dtype
    )

    q_all = [stacked_queries(q_ref, pl.ds(r * tree_len, tree_len), heads) for r in range(n_req)]
    tree_mask = (
        jnp.concatenate(
            [reach[r * tree_len : (r + 1) * tree_len] for r in range(n_req) for _ in range(heads)],
            axis=0,
        )
        > 0.5
    )
    s = nt_dot(jnp.concatenate(q_all, axis=0), tree_rows[:, :HEAD_SIZE]) * scale
    s = jnp.where(tree_mask, s, very_negative)
    m = jnp.max(s, axis=1, keepdims=True)
    w = jnp.where(tree_mask, jnp.exp(s - m), 0.0).astype(jnp.bfloat16)
    l = jnp.sum(w.astype(jnp.float32), axis=1, keepdims=True)
    a = jnp.dot(w, tree_rows[:, HEAD_SIZE:], preferred_element_type=jnp.float32)

    for r in range(n_req):
        rows = slice(r * stacked, (r + 1) * stacked)
        pages = [pool_ref[table_ref[r, k]] for k in range(LOCAL)]
        pages += [
            spill_ref[jnp.clip(table_ref[r, k] - spill_base, 0, spill_slots - 1)]
            for k in range(LOCAL, max_pages)
        ]
        blocks = [(m[rows], l[rows], a[rows])] + page_blocks(q_all[r], pages, 0, len_ref[r])
        _, total, accum = merge(blocks)
        att = (accum / total).astype(att_sc.dtype)
        for g in range(heads):
            att_sc[pl.ds(r * tree_len, tree_len), pl.ds(g * HEAD_SIZE, HEAD_SIZE)] = att[
                g * tree_len : (g + 1) * tree_len
            ]

    weight_copy.wait()
    proj_ref[...] = jnp.dot(
        att_sc[...], weight_vmem[...], preferred_element_type=jnp.float32
    ).astype(proj_ref.dtype)


def step(queries, tree_kv, page_pool, page_table, cache_len, parents, accepted, o_weight):
    requests, _ = parents.shape
    pool_slots = page_pool[:, 0]
    own_slots = requests * LOCAL
    ring = lax.axis_size("req")
    spill_source = pool_slots[own_slots:]
    spill = lax.ppermute(spill_source, "req", [((i + 1) % ring, i) for i in range(ring)])
    tree_rows = tree_kv[:, 0, :]
    smem = pl.BlockSpec(memory_space=pltpu.SMEM)
    vmem = pl.BlockSpec(memory_space=pltpu.VMEM)
    merged_call = pl.pallas_call(
        functools.partial(merged_kernel, own_slots),
        out_shape=(
            jax.ShapeDtypeStruct((queries.shape[0], o_weight.shape[1]), jnp.bfloat16),
            jax.ShapeDtypeStruct(tree_rows.shape, jnp.bfloat16),
        ),
        in_specs=[smem, smem, smem, vmem, vmem, vmem, vmem, vmem, pl.BlockSpec(memory_space=pl.ANY)],
        out_specs=(vmem, vmem),
        scratch_shapes=[
            pltpu.VMEM(o_weight.shape, o_weight.dtype),
            pltpu.VMEM(queries.shape, jnp.bfloat16),
            pltpu.SemaphoreType.DMA(()),
        ],
    )
    partial, kept = merged_call(
        page_table, cache_len, accepted, parents, queries, tree_rows, pool_slots, spill, o_weight
    )
    parts = lax.axis_size("tp")
    gathered = lax.all_to_all(partial, "tp", 0, 0, tiled=True)
    blocks = gathered.reshape(parts, partial.shape[0] // parts, partial.shape[1])
    summed = blocks[0].astype(jnp.float32)
    for i in range(1, parts):
        summed = summed + blocks[i].astype(jnp.float32)
    projected = summed.astype(jnp.bfloat16)
    return (projected, kept.reshape(kept.shape[0], 1, kept.shape[1]))


def solution(mesh):
    in_specs = (
        P("req", "tp"),
        P("req", "tp", None),
        P("req", "tp", None, None),
        P("req", None),
        P("req"),
        P("req", None),
        P("req"),
        P("tp", None),
    )
    out_specs = (P(("req", "tp"), None), P("req", "tp", None))
    return jax.shard_map(step, mesh=mesh, in_specs=in_specs, out_specs=out_specs, check_vma=False)
```

```python
import functools
import math

import jax
import jax.numpy as jnp
from jax import lax
from jax.experimental import pallas as pl
from jax.experimental.pallas import tpu as pltpu
from jax.sharding import PartitionSpec as P

HEAD_SIZE = 128
LOCAL = 2

very_negative = -1e30


def nt_dot(a, b):
    return lax.dot_general(a, b, (((1,), (1,)), ((), ())), preferred_element_type=jnp.float32)


def stacked_queries(q_ref, rows, heads):
    q = q_ref[rows, :]
    return jnp.concatenate(
        [q[:, g * HEAD_SIZE : (g + 1) * HEAD_SIZE] for g in range(heads)], axis=0
    )


def page_blocks(q_all, pages, first_page, length):
    page_len = pages[0].shape[0]
    keys = jnp.concatenate([page[:, :HEAD_SIZE] for page in pages], axis=0)
    lane = lax.broadcasted_iota(jnp.int32, (1, keys.shape[0]), 1)
    visible = (first_page * page_len + lane) < length
    scores = nt_dot(q_all, keys) * (1.0 / math.sqrt(HEAD_SIZE))
    scores = jnp.where(visible, scores, very_negative)
    blocks = []
    for k, page in enumerate(pages):
        cols = slice(k * page_len, (k + 1) * page_len)
        s = scores[:, cols]
        m = jnp.max(s, axis=1, keepdims=True)
        w = jnp.where(visible[:, cols], jnp.exp(s - m), 0.0).astype(jnp.bfloat16)
        l = jnp.sum(w.astype(jnp.float32), axis=1, keepdims=True)
        a = jnp.dot(w, page[:, HEAD_SIZE:], preferred_element_type=jnp.float32)
        blocks.append((m, l, a))
    return blocks


def merge(blocks):
    top = blocks[0][0]
    for m, _, _ in blocks[1:]:
        top = jnp.maximum(top, m)
    total = None
    accum = None
    for m, l, a in blocks:
        f = jnp.exp(m - top)
        total = f * l if total is None else total + f * l
        accum = f * a if accum is None else accum + f * a
    return top, total, accum


def local_kernel(
    table_ref, len_ref, leaf_ref, parents_ref, q_ref, tree_ref, pool_ref,
    kept_ref, ml_ref, a_ref,
):
    n_req, tree_len = parents_ref.shape
    nodes = n_req * tree_len
    heads = q_ref.shape[1] // HEAD_SIZE
    stacked = heads * tree_len
    scale = 1.0 / math.sqrt(HEAD_SIZE)
    sub = lax.broadcasted_iota(jnp.int32, (nodes, nodes), 0)
    lane = lax.broadcasted_iota(jnp.int32, (nodes, nodes), 1)
    eye = (sub == lane).astype(jnp.float32)
    squarings = (tree_len - 1).bit_length()

    parents = parents_ref[...].astype(jnp.float32)
    first = lax.broadcasted_iota(jnp.int32, parents.shape, 0).astype(jnp.float32) * tree_len
    parents = jnp.where(parents >= 0.0, parents + first, -1.0).astype(jnp.bfloat16)
    node = lax.broadcasted_iota(jnp.int32, (tree_len, nodes), 0)
    column = lax.broadcasted_iota(jnp.int32, (tree_len, nodes), 1)
    parent_row = None
    for r in range(n_req):
        place = (column == node + r * tree_len).astype(jnp.bfloat16)
        lhs = jnp.broadcast_to(parents[r : r + 1], (16, tree_len))
        placed = jnp.dot(lhs, place, preferred_element_type=jnp.float32)[0:1]
        parent_row = placed if parent_row is None else parent_row + placed

    rt = eye + (sub.astype(jnp.float32) == parent_row).astype(jnp.float32)
    for _ in range(squarings):
        rb = rt.astype(jnp.bfloat16)
        rt = jnp.minimum(jnp.dot(rb, rb, preferred_element_type=jnp.float32), 1.0)
    reach = nt_dot(eye.astype(jnp.bfloat16), rt.astype(jnp.bfloat16))

    depth = jnp.sum(rt, axis=0, keepdims=True) - 1.0
    slot = lax.broadcasted_iota(jnp.int32, (tree_len, nodes), 0).astype(jnp.float32)
    selectors = []
    for r in range(n_req):
        leaf = r * tree_len + leaf_ref[r]
        kept_mask = jnp.sum(jnp.where(sub == leaf, reach, 0.0), axis=0, keepdims=True)
        selectors.append(jnp.where((slot == depth) & (kept_mask > 0.5), 1.0, 0.0))
    selector = jnp.concatenate(selectors, axis=0).astype(jnp.bfloat16)
    tree_rows = tree_ref[...]
    kept_ref[...] = jnp.dot(selector, tree_rows, preferred_element_type=jnp.float32).astype(
        kept_ref.dtype
    )

    q_all = [stacked_queries(q_ref, pl.ds(r * tree_len, tree_len), heads) for r in range(n_req)]
    tree_mask = (
        jnp.concatenate(
            [reach[r * tree_len : (r + 1) * tree_len] for r in range(n_req) for _ in range(heads)],
            axis=0,
        )
        > 0.5
    )
    s = nt_dot(jnp.concatenate(q_all, axis=0), tree_rows[:, :HEAD_SIZE]) * scale
    s = jnp.where(tree_mask, s, very_negative)
    m = jnp.max(s, axis=1, keepdims=True)
    w = jnp.where(tree_mask, jnp.exp(s - m), 0.0).astype(jnp.bfloat16)
    l = jnp.sum(w.astype(jnp.float32), axis=1, keepdims=True)
    a = jnp.dot(w, tree_rows[:, HEAD_SIZE:], preferred_element_type=jnp.float32)

    state_lane = lax.broadcasted_iota(jnp.int32, (stacked, HEAD_SIZE), 1)
    for r in range(n_req):
        rows = slice(r * stacked, (r + 1) * stacked)
        pages = [pool_ref[table_ref[r, k]] for k in range(LOCAL)]
        blocks = [(m[rows], l[rows], a[rows])] + page_blocks(q_all[r], pages, 0, len_ref[r])
        top, total, accum = merge(blocks)
        ml_ref[r] = jnp.where(state_lane == 0, top, jnp.where(state_lane == 1, total, 0.0))
        a_ref[r] = accum


def spill_kernel(
    spill_base, table_ref, len_ref, ml_ref, a_ref, q_ref, spill_ref, weight_hbm,
    proj_ref, weight_vmem, att_sc, weight_sem,
):
    weight_copy = pltpu.make_async_copy(weight_hbm, weight_vmem, weight_sem)
    weight_copy.start()
    n_req, tree_len = table_ref.shape[0], q_ref.shape[0] // table_ref.shape[0]
    heads = q_ref.shape[1] // HEAD_SIZE
    max_pages = table_ref.shape[1]
    spill_slots = spill_ref.shape[0]
    page_len = spill_ref.shape[1]
    for r in range(n_req):
        rows = pl.ds(r * tree_len, tree_len)
        length = len_ref[r]

        def write(att):
            for g in range(heads):
                att_sc[rows, pl.ds(g * HEAD_SIZE, HEAD_SIZE)] = att[g * tree_len : (g + 1) * tree_len]

        @pl.when(length > LOCAL * page_len)
        def _():
            q_all = stacked_queries(q_ref, rows, heads)
            pages = [
                spill_ref[jnp.clip(table_ref[r, k] - spill_base, 0, spill_slots - 1)]
                for k in range(LOCAL, max_pages)
            ]
            ml = ml_ref[r]
            state = (ml[:, 0:1], ml[:, 1:2], a_ref[r])
            _, total, accum = merge([state] + page_blocks(q_all, pages, LOCAL, length))
            write((accum / total).astype(att_sc.dtype))

        @pl.when(length <= LOCAL * page_len)
        def _():
            ml = ml_ref[r]
            write((a_ref[r] / ml[:, 1:2]).astype(att_sc.dtype))

    weight_copy.wait()
    proj_ref[...] = jnp.dot(
        att_sc[...], weight_vmem[...], preferred_element_type=jnp.float32
    ).astype(proj_ref.dtype)


def step(queries, tree_kv, page_pool, page_table, cache_len, parents, accepted, o_weight):
    requests, tree_len = parents.shape
    heads = queries.shape[1] // HEAD_SIZE
    pool_slots = page_pool[:, 0]
    own_slots = requests * LOCAL
    ring = lax.axis_size("req")
    spill_source = pool_slots[own_slots:]
    spill = lax.ppermute(spill_source, "req", [((i + 1) % ring, i) for i in range(ring)])
    tree_rows = tree_kv[:, 0, :]
    smem = pl.BlockSpec(memory_space=pltpu.SMEM)
    vmem = pl.BlockSpec(memory_space=pltpu.VMEM)
    stacked = heads * tree_len
    local_call = pl.pallas_call(
        local_kernel,
        out_shape=(
            jax.ShapeDtypeStruct(tree_rows.shape, jnp.bfloat16),
            jax.ShapeDtypeStruct((requests, stacked, HEAD_SIZE), jnp.float32),
            jax.ShapeDtypeStruct((requests, stacked, HEAD_SIZE), jnp.float32),
        ),
        in_specs=[smem, smem, smem, vmem, vmem, vmem, vmem],
        out_specs=(vmem, vmem, vmem),
    )
    kept, packed, accum = local_call(
        page_table, cache_len, accepted, parents, queries, tree_rows, pool_slots
    )
    partial = pl.pallas_call(
        functools.partial(spill_kernel, own_slots),
        out_shape=jax.ShapeDtypeStruct((queries.shape[0], o_weight.shape[1]), jnp.bfloat16),
        in_specs=[smem, smem, vmem, vmem, vmem, vmem, pl.BlockSpec(memory_space=pl.ANY)],
        out_specs=vmem,
        scratch_shapes=[
            pltpu.VMEM(o_weight.shape, o_weight.dtype),
            pltpu.VMEM(queries.shape, jnp.bfloat16),
            pltpu.SemaphoreType.DMA(()),
        ],
    )(page_table, cache_len, packed, accum, queries, spill, o_weight)

    parts = lax.axis_size("tp")
    gathered = lax.all_to_all(partial, "tp", 0, 0, tiled=True)
    blocks = gathered.reshape(parts, partial.shape[0] // parts, partial.shape[1])
    summed = blocks[0].astype(jnp.float32)
    for i in range(1, parts):
        summed = summed + blocks[i].astype(jnp.float32)
    projected = summed.astype(jnp.bfloat16)
    return (projected, kept.reshape(kept.shape[0], 1, kept.shape[1]))


def solution(mesh):
    in_specs = (
        P("req", "tp"),
        P("req", "tp", None),
        P("req", "tp", None, None),
        P("req", None),
        P("req"),
        P("req", None),
        P("req"),
        P("tp", None),
    )
    out_specs = (P(("req", "tp"), None), P("req", "tp", None))
    return jax.shard_map(step, mesh=mesh, in_specs=in_specs, out_specs=out_specs, check_vma=False)
```

```python
import functools
import math

import jax
import jax.numpy as jnp
from jax import lax
from jax.experimental import pallas as pl
from jax.experimental.pallas import tpu as pltpu
from jax.sharding import PartitionSpec as P

HEAD_SIZE = 128
LOCAL = 2

very_negative = -1e30


def nt_dot(a, b):
    return lax.dot_general(a, b, (((1,), (1,)), ((), ())), preferred_element_type=jnp.float32)


def stacked_queries(q_ref, rows, heads):
    q = q_ref[rows, :]
    return jnp.concatenate(
        [q[:, g * HEAD_SIZE : (g + 1) * HEAD_SIZE] for g in range(heads)], axis=0
    )


def page_blocks(q_all, pages, first_page, length):
    page_len = pages[0].shape[0]
    keys = jnp.concatenate([page[:, :HEAD_SIZE] for page in pages], axis=0)
    lane = lax.broadcasted_iota(jnp.int32, (1, keys.shape[0]), 1)
    visible = (first_page * page_len + lane) < length
    scores = nt_dot(q_all, keys) * (1.0 / math.sqrt(HEAD_SIZE))
    scores = jnp.where(visible, scores, very_negative)
    blocks = []
    for k, page in enumerate(pages):
        cols = slice(k * page_len, (k + 1) * page_len)
        s = scores[:, cols]
        m = jnp.max(s, axis=1, keepdims=True)
        w = jnp.where(visible[:, cols], jnp.exp(s - m), 0.0).astype(jnp.bfloat16)
        l = jnp.sum(w.astype(jnp.float32), axis=1, keepdims=True)
        a = jnp.dot(w, page[:, HEAD_SIZE:], preferred_element_type=jnp.float32)
        blocks.append((m, l, a))
    return blocks


def merge(blocks):
    top = blocks[0][0]
    for m, _, _ in blocks[1:]:
        top = jnp.maximum(top, m)
    total = None
    accum = None
    for m, l, a in blocks:
        f = jnp.exp(m - top)
        total = f * l if total is None else total + f * l
        accum = f * a if accum is None else accum + f * a
    return top, total, accum


def local_kernel(
    table_ref, len_ref, leaf_ref, parents_ref, q_ref, tree_ref, pool_ref,
    kept_ref, ml_ref, a_ref,
):
    n_req, tree_len = parents_ref.shape
    nodes = n_req * tree_len
    heads = q_ref.shape[1] // HEAD_SIZE
    stacked = heads * tree_len
    scale = 1.0 / math.sqrt(HEAD_SIZE)
    sub = lax.broadcasted_iota(jnp.int32, (nodes, nodes), 0)
    lane = lax.broadcasted_iota(jnp.int32, (nodes, nodes), 1)
    eye = (sub == lane).astype(jnp.float32)
    squarings = (tree_len - 1).bit_length()

    parents = parents_ref[...].astype(jnp.float32)
    first = lax.broadcasted_iota(jnp.int32, parents.shape, 0).astype(jnp.float32) * tree_len
    parents = jnp.where(parents >= 0.0, parents + first, -1.0).astype(jnp.bfloat16)
    node = lax.broadcasted_iota(jnp.int32, (tree_len, nodes), 0)
    column = lax.broadcasted_iota(jnp.int32, (tree_len, nodes), 1)
    parent_row = None
    for r in range(n_req):
        place = (column == node + r * tree_len).astype(jnp.bfloat16)
        lhs = jnp.broadcast_to(parents[r : r + 1], (16, tree_len))
        placed = jnp.dot(lhs, place, preferred_element_type=jnp.float32)[0:1]
        parent_row = placed if parent_row is None else parent_row + placed

    rt = eye + (sub.astype(jnp.float32) == parent_row).astype(jnp.float32)
    for _ in range(squarings):
        rb = rt.astype(jnp.bfloat16)
        rt = jnp.minimum(jnp.dot(rb, rb, preferred_element_type=jnp.float32), 1.0)
    reach = nt_dot(eye.astype(jnp.bfloat16), rt.astype(jnp.bfloat16))

    depth = jnp.sum(rt, axis=0, keepdims=True) - 1.0
    slot = lax.broadcasted_iota(jnp.int32, (tree_len, nodes), 0).astype(jnp.float32)
    selectors = []
    for r in range(n_req):
        leaf = r * tree_len + leaf_ref[r]
        kept_mask = jnp.sum(jnp.where(sub == leaf, reach, 0.0), axis=0, keepdims=True)
        selectors.append(jnp.where((slot == depth) & (kept_mask > 0.5), 1.0, 0.0))
    selector = jnp.concatenate(selectors, axis=0).astype(jnp.bfloat16)
    tree_rows = tree_ref[...]
    kept_ref[...] = jnp.dot(selector, tree_rows, preferred_element_type=jnp.float32).astype(
        kept_ref.dtype
    )

    q_all = [stacked_queries(q_ref, pl.ds(r * tree_len, tree_len), heads) for r in range(n_req)]
    tree_mask = (
        jnp.concatenate(
            [reach[r * tree_len : (r + 1) * tree_len] for r in range(n_req) for _ in range(heads)],
            axis=0,
        )
        > 0.5
    )
    s = nt_dot(jnp.concatenate(q_all, axis=0), tree_rows[:, :HEAD_SIZE]) * scale
    s = jnp.where(tree_mask, s, very_negative)
    m = jnp.max(s, axis=1, keepdims=True)
    w = jnp.where(tree_mask, jnp.exp(s - m), 0.0).astype(jnp.bfloat16)
    l = jnp.sum(w.astype(jnp.float32), axis=1, keepdims=True)
    a = jnp.dot(w, tree_rows[:, HEAD_SIZE:], preferred_element_type=jnp.float32)

    state_lane = lax.broadcasted_iota(jnp.int32, (stacked, HEAD_SIZE), 1)
    for r in range(n_req):
        rows = slice(r * stacked, (r + 1) * stacked)
        pages = [pool_ref[table_ref[r, k]] for k in range(LOCAL)]
        blocks = [(m[rows], l[rows], a[rows])] + page_blocks(q_all[r], pages, 0, len_ref[r])
        top, total, accum = merge(blocks)
        ml_ref[r] = jnp.where(state_lane == 0, top, jnp.where(state_lane == 1, total, 0.0))
        a_ref[r] = accum


def spill_kernel(
    spill_base, table_ref, len_ref, ml_ref, a_ref, q_ref, spill_ref, weight_hbm,
    proj_ref, weight_vmem, att_sc, weight_sem,
):
    weight_copy = pltpu.make_async_copy(weight_hbm, weight_vmem, weight_sem)
    weight_copy.start()
    n_req, tree_len = table_ref.shape[0], q_ref.shape[0] // table_ref.shape[0]
    heads = q_ref.shape[1] // HEAD_SIZE
    max_pages = table_ref.shape[1]
    spill_slots = spill_ref.shape[0]
    for r in range(n_req):
        rows = pl.ds(r * tree_len, tree_len)
        q_all = stacked_queries(q_ref, rows, heads)
        pages = [
            spill_ref[jnp.clip(table_ref[r, k] - spill_base, 0, spill_slots - 1)]
            for k in range(LOCAL, max_pages)
        ]
        ml = ml_ref[r]
        state = (ml[:, 0:1], ml[:, 1:2], a_ref[r])
        _, total, accum = merge([state] + page_blocks(q_all, pages, LOCAL, len_ref[r]))
        att = (accum / total).astype(att_sc.dtype)
        for g in range(heads):
            att_sc[rows, pl.ds(g * HEAD_SIZE, HEAD_SIZE)] = att[g * tree_len : (g + 1) * tree_len]

    weight_copy.wait()
    proj_ref[...] = jnp.dot(
        att_sc[...], weight_vmem[...], preferred_element_type=jnp.float32
    ).astype(proj_ref.dtype)


def step(queries, tree_kv, page_pool, page_table, cache_len, parents, accepted, o_weight):
    requests, tree_len = parents.shape
    heads = queries.shape[1] // HEAD_SIZE
    pool_slots = page_pool[:, 0]
    own_slots = requests * LOCAL
    ring = lax.axis_size("req")
    spill_source = pool_slots[own_slots:]
    spill = lax.ppermute(spill_source, "req", [((i + 1) % ring, i) for i in range(ring)])
    tree_rows = tree_kv[:, 0, :]
    smem = pl.BlockSpec(memory_space=pltpu.SMEM)
    vmem = pl.BlockSpec(memory_space=pltpu.VMEM)
    stacked = heads * tree_len
    local_call = pl.pallas_call(
        local_kernel,
        out_shape=(
            jax.ShapeDtypeStruct(tree_rows.shape, jnp.bfloat16),
            jax.ShapeDtypeStruct((requests, stacked, HEAD_SIZE), jnp.float32),
            jax.ShapeDtypeStruct((requests, stacked, HEAD_SIZE), jnp.float32),
        ),
        in_specs=[smem, smem, smem, vmem, vmem, vmem, vmem],
        out_specs=(vmem, vmem, vmem),
    )
    kept, packed, accum = local_call(
        page_table, cache_len, accepted, parents, queries, tree_rows, pool_slots
    )
    partial = pl.pallas_call(
        functools.partial(spill_kernel, own_slots),
        out_shape=jax.ShapeDtypeStruct((queries.shape[0], o_weight.shape[1]), jnp.bfloat16),
        in_specs=[smem, smem, vmem, vmem, vmem, vmem, pl.BlockSpec(memory_space=pl.ANY)],
        out_specs=vmem,
        scratch_shapes=[
            pltpu.VMEM(o_weight.shape, o_weight.dtype),
            pltpu.VMEM(queries.shape, jnp.bfloat16),
            pltpu.SemaphoreType.DMA(()),
        ],
    )(page_table, cache_len, packed, accum, queries, spill, o_weight)

    parts = lax.axis_size("tp")
    gathered = lax.all_to_all(partial, "tp", 0, 0, tiled=True)
    blocks = gathered.reshape(parts, partial.shape[0] // parts, partial.shape[1])
    summed = blocks[0].astype(jnp.float32)
    for i in range(1, parts):
        summed = summed + blocks[i].astype(jnp.float32)
    projected = summed.astype(jnp.bfloat16)
    return (projected, kept.reshape(kept.shape[0], 1, kept.shape[1]))


def solution(mesh):
    in_specs = (
        P("req", "tp"),
        P("req", "tp", None),
        P("req", "tp", None, None),
        P("req", None),
        P("req"),
        P("req", None),
        P("req"),
        P("tp", None),
    )
    out_specs = (P(("req", "tp"), None), P("req", "tp", None))
    return jax.shard_map(step, mesh=mesh, in_specs=in_specs, out_specs=out_specs, check_vma=False)
```

```python
import functools
import math

import jax
import jax.numpy as jnp
from jax import lax
from jax.experimental import pallas as pl
from jax.experimental.pallas import tpu as pltpu
from jax.sharding import PartitionSpec as P

HEAD_SIZE = 128
LOCAL = 2

very_negative = -1e30


def nt_dot(a, b):
    return lax.dot_general(a, b, (((1,), (1,)), ((), ())), preferred_element_type=jnp.float32)


def stacked_queries(q_ref, rows, heads):
    q = q_ref[rows, :]
    return jnp.concatenate(
        [q[:, g * HEAD_SIZE : (g + 1) * HEAD_SIZE] for g in range(heads)], axis=0
    )


def page_blocks(q_all, pages, first_page, length):
    page_len = pages[0].shape[0]
    keys = jnp.concatenate([page[:, :HEAD_SIZE] for page in pages], axis=0)
    lane = lax.broadcasted_iota(jnp.int32, (1, keys.shape[0]), 1)
    visible = (first_page * page_len + lane) < length
    scores = nt_dot(q_all, keys) * (1.0 / math.sqrt(HEAD_SIZE))
    scores = jnp.where(visible, scores, very_negative)
    blocks = []
    for k, page in enumerate(pages):
        cols = slice(k * page_len, (k + 1) * page_len)
        s = scores[:, cols]
        m = jnp.max(s, axis=1, keepdims=True)
        w = jnp.where(visible[:, cols], jnp.exp(s - m), 0.0).astype(jnp.bfloat16)
        l = jnp.sum(w.astype(jnp.float32), axis=1, keepdims=True)
        a = jnp.dot(w, page[:, HEAD_SIZE:], preferred_element_type=jnp.float32)
        blocks.append((m, l, a))
    return blocks


def merge(blocks):
    top = blocks[0][0]
    for m, _, _ in blocks[1:]:
        top = jnp.maximum(top, m)
    total = None
    accum = None
    for m, l, a in blocks:
        f = jnp.exp(m - top)
        total = f * l if total is None else total + f * l
        accum = f * a if accum is None else accum + f * a
    return top, total, accum


def local_kernel(
    table_ref, len_ref, leaf_ref, parents_ref, q_ref, tree_ref, pool_ref,
    kept_ref, ml_ref, a_ref,
):
    n_req, tree_len = parents_ref.shape
    nodes = n_req * tree_len
    heads = q_ref.shape[1] // HEAD_SIZE
    stacked = heads * tree_len
    scale = 1.0 / math.sqrt(HEAD_SIZE)
    sub = lax.broadcasted_iota(jnp.int32, (nodes, nodes), 0)
    lane = lax.broadcasted_iota(jnp.int32, (nodes, nodes), 1)
    eye = (sub == lane).astype(jnp.float32)
    squarings = (tree_len - 1).bit_length()

    parents = parents_ref[...].astype(jnp.float32)
    first = lax.broadcasted_iota(jnp.int32, parents.shape, 0).astype(jnp.float32) * tree_len
    parents = jnp.where(parents >= 0.0, parents + first, -1.0).astype(jnp.bfloat16)
    node = lax.broadcasted_iota(jnp.int32, (tree_len, nodes), 0)
    column = lax.broadcasted_iota(jnp.int32, (tree_len, nodes), 1)
    parent_row = None
    for r in range(n_req):
        place = (column == node + r * tree_len).astype(jnp.bfloat16)
        lhs = jnp.broadcast_to(parents[r : r + 1], (16, tree_len))
        placed = jnp.dot(lhs, place, preferred_element_type=jnp.float32)[0:1]
        parent_row = placed if parent_row is None else parent_row + placed

    rt = eye + (sub.astype(jnp.float32) == parent_row).astype(jnp.float32)
    for _ in range(squarings):
        rb = rt.astype(jnp.bfloat16)
        rt = jnp.minimum(jnp.dot(rb, rb, preferred_element_type=jnp.float32), 1.0)
    reach = nt_dot(eye.astype(jnp.bfloat16), rt.astype(jnp.bfloat16))

    depth = jnp.sum(rt, axis=0, keepdims=True) - 1.0
    slot = lax.broadcasted_iota(jnp.int32, (tree_len, nodes), 0).astype(jnp.float32)
    selectors = []
    for r in range(n_req):
        leaf = r * tree_len + leaf_ref[r]
        kept_mask = jnp.sum(jnp.where(sub == leaf, reach, 0.0), axis=0, keepdims=True)
        selectors.append(jnp.where((slot == depth) & (kept_mask > 0.5), 1.0, 0.0))
    selector = jnp.concatenate(selectors, axis=0).astype(jnp.bfloat16)
    tree_rows = tree_ref[...]
    kept_ref[...] = jnp.dot(selector, tree_rows, preferred_element_type=jnp.float32).astype(
        kept_ref.dtype
    )

    q_all = [stacked_queries(q_ref, pl.ds(r * tree_len, tree_len), heads) for r in range(n_req)]
    tree_mask = (
        jnp.concatenate(
            [reach[r * tree_len : (r + 1) * tree_len] for r in range(n_req) for _ in range(heads)],
            axis=0,
        )
        > 0.5
    )
    s = nt_dot(jnp.concatenate(q_all, axis=0), tree_rows[:, :HEAD_SIZE]) * scale
    s = jnp.where(tree_mask, s, very_negative)
    m = jnp.max(s, axis=1, keepdims=True)
    w = jnp.where(tree_mask, jnp.exp(s - m), 0.0).astype(jnp.bfloat16)
    l = jnp.sum(w.astype(jnp.float32), axis=1, keepdims=True)
    a = jnp.dot(w, tree_rows[:, HEAD_SIZE:], preferred_element_type=jnp.float32)

    state_lane = lax.broadcasted_iota(jnp.int32, (stacked, HEAD_SIZE), 1)
    for r in range(n_req):
        rows = slice(r * stacked, (r + 1) * stacked)
        pages = [pool_ref[table_ref[r, k]] for k in range(LOCAL)]
        blocks = [(m[rows], l[rows], a[rows])] + page_blocks(q_all[r], pages, 0, len_ref[r])
        top, total, accum = merge(blocks)
        ml_ref[r] = jnp.where(state_lane == 0, top, jnp.where(state_lane == 1, total, 0.0))
        a_ref[r] = accum


def spill_kernel(
    spill_base, table_ref, len_ref, ml_ref, a_ref, q_ref, spill_ref, weight_hbm,
    proj_ref, weight_vmem, att_sc, weight_sem,
):
    weight_copy = pltpu.make_async_copy(weight_hbm, weight_vmem, weight_sem)
    weight_copy.start()
    n_req, tree_len = table_ref.shape[0], q_ref.shape[0] // table_ref.shape[0]
    heads = q_ref.shape[1] // HEAD_SIZE
    max_pages = table_ref.shape[1]
    spill_slots = spill_ref.shape[0]
    for r in range(n_req):
        rows = pl.ds(r * tree_len, tree_len)
        q_all = stacked_queries(q_ref, rows, heads)
        pages = [
            spill_ref[jnp.clip(table_ref[r, k] - spill_base, 0, spill_slots - 1)]
            for k in range(LOCAL, max_pages)
        ]
        ml = ml_ref[r]
        state = (ml[:, 0:1], ml[:, 1:2], a_ref[r])
        _, total, accum = merge([state] + page_blocks(q_all, pages, LOCAL, len_ref[r]))
        att = (accum / total).astype(att_sc.dtype)
        for g in range(heads):
            att_sc[rows, pl.ds(g * HEAD_SIZE, HEAD_SIZE)] = att[g * tree_len : (g + 1) * tree_len]

    weight_copy.wait()
    proj_ref[...] = jnp.dot(
        att_sc[...], weight_vmem[...], preferred_element_type=jnp.float32
    ).astype(proj_ref.dtype)


def slot_copy_kernel(first, pool_hbm, out_hbm, sem):
    copy = pltpu.make_async_copy(pool_hbm.at[pl.ds(first, out_hbm.shape[0])], out_hbm, sem)
    copy.start()
    copy.wait()


def step(queries, tree_kv, page_pool, page_table, cache_len, parents, accepted, o_weight):
    requests, tree_len = parents.shape
    heads = queries.shape[1] // HEAD_SIZE
    pool_slots = page_pool[:, 0]
    own_slots = requests * LOCAL
    ring = lax.axis_size("req")
    any_space = pl.BlockSpec(memory_space=pl.ANY)
    spill_source = pl.pallas_call(
        functools.partial(slot_copy_kernel, own_slots),
        out_shape=jax.ShapeDtypeStruct(
            (pool_slots.shape[0] - own_slots,) + pool_slots.shape[1:], pool_slots.dtype
        ),
        in_specs=[any_space],
        out_specs=any_space,
        scratch_shapes=[pltpu.SemaphoreType.DMA(())],
    )(pool_slots)
    spill = lax.ppermute(spill_source, "req", [((i + 1) % ring, i) for i in range(ring)])
    tree_rows = tree_kv[:, 0, :]
    smem = pl.BlockSpec(memory_space=pltpu.SMEM)
    vmem = pl.BlockSpec(memory_space=pltpu.VMEM)
    stacked = heads * tree_len
    local_call = pl.pallas_call(
        local_kernel,
        out_shape=(
            jax.ShapeDtypeStruct(tree_rows.shape, jnp.bfloat16),
            jax.ShapeDtypeStruct((requests, stacked, HEAD_SIZE), jnp.float32),
            jax.ShapeDtypeStruct((requests, stacked, HEAD_SIZE), jnp.float32),
        ),
        in_specs=[smem, smem, smem, vmem, vmem, vmem, vmem],
        out_specs=(vmem, vmem, vmem),
    )
    kept, packed, accum = local_call(
        page_table, cache_len, accepted, parents, queries, tree_rows, pool_slots
    )
    partial = pl.pallas_call(
        functools.partial(spill_kernel, own_slots),
        out_shape=jax.ShapeDtypeStruct((queries.shape[0], o_weight.shape[1]), jnp.bfloat16),
        in_specs=[smem, smem, vmem, vmem, vmem, vmem, pl.BlockSpec(memory_space=pl.ANY)],
        out_specs=vmem,
        scratch_shapes=[
            pltpu.VMEM(o_weight.shape, o_weight.dtype),
            pltpu.VMEM(queries.shape, jnp.bfloat16),
            pltpu.SemaphoreType.DMA(()),
        ],
    )(page_table, cache_len, packed, accum, queries, spill, o_weight)

    parts = lax.axis_size("tp")
    gathered = lax.all_to_all(partial, "tp", 0, 0, tiled=True)
    blocks = gathered.reshape(parts, partial.shape[0] // parts, partial.shape[1])
    summed = blocks[0].astype(jnp.float32)
    for i in range(1, parts):
        summed = summed + blocks[i].astype(jnp.float32)
    projected = summed.astype(jnp.bfloat16)
    return (projected, kept.reshape(kept.shape[0], 1, kept.shape[1]))


def solution(mesh):
    in_specs = (
        P("req", "tp"),
        P("req", "tp", None),
        P("req", "tp", None, None),
        P("req", None),
        P("req"),
        P("req", None),
        P("req"),
        P("tp", None),
    )
    out_specs = (P(("req", "tp"), None), P("req", "tp", None))
    return jax.shard_map(step, mesh=mesh, in_specs=in_specs, out_specs=out_specs, check_vma=False)
```

```python
import functools
import math

import jax
import jax.numpy as jnp
from jax import lax
from jax.experimental import pallas as pl
from jax.experimental.pallas import tpu as pltpu
from jax.sharding import PartitionSpec as P

HEAD_SIZE = 128
LOCAL = 2

very_negative = -1e30


def nt_dot(a, b):
    return lax.dot_general(a, b, (((1,), (1,)), ((), ())), preferred_element_type=jnp.float32)


def stacked_queries(q_ref, rows, heads):
    q = q_ref[rows, :]
    return jnp.concatenate(
        [q[:, g * HEAD_SIZE : (g + 1) * HEAD_SIZE] for g in range(heads)], axis=0
    )


def page_blocks(q_all, pages, first_page, length):
    page_len = pages[0].shape[0]
    keys = jnp.concatenate([page[:, :HEAD_SIZE] for page in pages], axis=0)
    lane = lax.broadcasted_iota(jnp.int32, (1, keys.shape[0]), 1)
    visible = (first_page * page_len + lane) < length
    scores = nt_dot(q_all, keys) * (1.0 / math.sqrt(HEAD_SIZE))
    scores = jnp.where(visible, scores, very_negative)
    blocks = []
    for k, page in enumerate(pages):
        cols = slice(k * page_len, (k + 1) * page_len)
        s = scores[:, cols]
        m = jnp.max(s, axis=1, keepdims=True)
        w = jnp.exp(s - m).astype(jnp.bfloat16)
        l = jnp.sum(w.astype(jnp.float32), axis=1, keepdims=True)
        a = jnp.dot(w, page[:, HEAD_SIZE:], preferred_element_type=jnp.float32)
        blocks.append((m, l, a))
    return blocks


def merge(blocks):
    top = blocks[0][0]
    for m, _, _ in blocks[1:]:
        top = jnp.maximum(top, m)
    total = None
    accum = None
    for m, l, a in blocks:
        f = jnp.exp(m - top)
        total = f * l if total is None else total + f * l
        accum = f * a if accum is None else accum + f * a
    return top, total, accum


def local_kernel(
    table_ref, len_ref, leaf_ref, parents_ref, q_ref, tree_ref, pool_ref,
    kept_ref, ml_ref, a_ref, qs_ref,
):
    n_req, tree_len = parents_ref.shape
    nodes = n_req * tree_len
    heads = q_ref.shape[1] // HEAD_SIZE
    stacked = heads * tree_len
    scale = 1.0 / math.sqrt(HEAD_SIZE)
    sub = lax.broadcasted_iota(jnp.int32, (nodes, nodes), 0)
    lane = lax.broadcasted_iota(jnp.int32, (nodes, nodes), 1)
    eye = (sub == lane).astype(jnp.float32)
    squarings = (tree_len - 1).bit_length()

    parents = parents_ref[...].astype(jnp.float32)
    first = lax.broadcasted_iota(jnp.int32, parents.shape, 0).astype(jnp.float32) * tree_len
    parents = jnp.where(parents >= 0.0, parents + first, -1.0).astype(jnp.bfloat16)
    node = lax.broadcasted_iota(jnp.int32, (tree_len, nodes), 0)
    column = lax.broadcasted_iota(jnp.int32, (tree_len, nodes), 1)
    parent_row = None
    for r in range(n_req):
        place = (column == node + r * tree_len).astype(jnp.bfloat16)
        lhs = jnp.broadcast_to(parents[r : r + 1], (16, tree_len))
        placed = jnp.dot(lhs, place, preferred_element_type=jnp.float32)[0:1]
        parent_row = placed if parent_row is None else parent_row + placed

    rt = eye + (sub.astype(jnp.float32) == parent_row).astype(jnp.float32)
    for _ in range(squarings):
        rb = rt.astype(jnp.bfloat16)
        rt = jnp.minimum(jnp.dot(rb, rb, preferred_element_type=jnp.float32), 1.0)
    reach = nt_dot(eye.astype(jnp.bfloat16), rt.astype(jnp.bfloat16))

    depth = jnp.sum(rt, axis=0, keepdims=True) - 1.0
    slot = lax.broadcasted_iota(jnp.int32, (tree_len, nodes), 0).astype(jnp.float32)
    selectors = []
    for r in range(n_req):
        leaf = r * tree_len + leaf_ref[r]
        kept_mask = jnp.sum(jnp.where(sub == leaf, reach, 0.0), axis=0, keepdims=True)
        selectors.append(jnp.where((slot == depth) & (kept_mask > 0.5), 1.0, 0.0))
    selector = jnp.concatenate(selectors, axis=0).astype(jnp.bfloat16)
    tree_rows = tree_ref[...]
    kept_ref[...] = jnp.dot(selector, tree_rows, preferred_element_type=jnp.float32).astype(
        kept_ref.dtype
    )

    q_all = [stacked_queries(q_ref, pl.ds(r * tree_len, tree_len), heads) for r in range(n_req)]
    for r in range(n_req):
        qs_ref[r] = q_all[r]
    tree_mask = (
        jnp.concatenate(
            [reach[r * tree_len : (r + 1) * tree_len] for r in range(n_req) for _ in range(heads)],
            axis=0,
        )
        > 0.5
    )
    s = nt_dot(jnp.concatenate(q_all, axis=0), tree_rows[:, :HEAD_SIZE]) * scale
    s = jnp.where(tree_mask, s, very_negative)
    m = jnp.max(s, axis=1, keepdims=True)
    w = jnp.exp(s - m).astype(jnp.bfloat16)
    l = jnp.sum(w.astype(jnp.float32), axis=1, keepdims=True)
    a = jnp.dot(w, tree_rows[:, HEAD_SIZE:], preferred_element_type=jnp.float32)

    state_lane = lax.broadcasted_iota(jnp.int32, (stacked, HEAD_SIZE), 1)
    for r in range(n_req):
        rows = slice(r * stacked, (r + 1) * stacked)
        pages = [pool_ref[table_ref[r, k]] for k in range(LOCAL)]
        blocks = [(m[rows], l[rows], a[rows])] + page_blocks(q_all[r], pages, 0, len_ref[r])
        top, total, accum = merge(blocks)
        ml_ref[r] = jnp.where(state_lane == 0, top, jnp.where(state_lane == 1, total, 0.0))
        a_ref[r] = accum


def spill_kernel(
    spill_base, table_ref, len_ref, ml_hbm, a_hbm, q_hbm, spill_hbm, weight_hbm,
    proj_ref, ml_ref, a_ref, q_ref, spill_ref, weight_vmem, att_sc, sems,
):
    copies = [
        pltpu.make_async_copy(src, dst, sems.at[i])
        for i, (src, dst) in enumerate(
            [(q_hbm, q_ref), (spill_hbm, spill_ref), (ml_hbm, ml_ref), (a_hbm, a_ref),
             (weight_hbm, weight_vmem)]
        )
    ]
    for copy in copies:
        copy.start()
    n_req, tree_len = table_ref.shape[0], att_sc.shape[0] // table_ref.shape[0]
    heads = att_sc.shape[1] // HEAD_SIZE
    max_pages = table_ref.shape[1]
    spill_slots = spill_ref.shape[0]
    copies[0].wait()
    copies[1].wait()
    blocks = []
    for r in range(n_req):
        pages = [
            spill_ref[jnp.clip(table_ref[r, k] - spill_base, 0, spill_slots - 1)]
            for k in range(LOCAL, max_pages)
        ]
        blocks.append(page_blocks(q_ref[r], pages, LOCAL, len_ref[r]))
    copies[2].wait()
    copies[3].wait()
    for r in range(n_req):
        rows = pl.ds(r * tree_len, tree_len)
        ml = ml_ref[r]
        state = (ml[:, 0:1], ml[:, 1:2], a_ref[r])
        _, total, accum = merge([state] + blocks[r])
        att = (accum / total).astype(att_sc.dtype)
        for g in range(heads):
            att_sc[rows, pl.ds(g * HEAD_SIZE, HEAD_SIZE)] = att[g * tree_len : (g + 1) * tree_len]

    copies[4].wait()
    proj_ref[...] = jnp.dot(
        att_sc[...], weight_vmem[...], preferred_element_type=jnp.float32
    ).astype(proj_ref.dtype)


def step(queries, tree_kv, page_pool, page_table, cache_len, parents, accepted, o_weight):
    requests, tree_len = parents.shape
    heads = queries.shape[1] // HEAD_SIZE
    pool_slots = page_pool[:, 0]
    own_slots = requests * LOCAL
    ring = lax.axis_size("req")
    spill_source = pool_slots[own_slots:]
    spill = lax.ppermute(spill_source, "req", [((i + 1) % ring, i) for i in range(ring)])
    tree_rows = tree_kv[:, 0, :]
    smem = pl.BlockSpec(memory_space=pltpu.SMEM)
    vmem = pl.BlockSpec(memory_space=pltpu.VMEM)
    stacked = heads * tree_len
    local_call = pl.pallas_call(
        local_kernel,
        out_shape=(
            jax.ShapeDtypeStruct(tree_rows.shape, jnp.bfloat16),
            jax.ShapeDtypeStruct((requests, stacked, HEAD_SIZE), jnp.float32),
            jax.ShapeDtypeStruct((requests, stacked, HEAD_SIZE), jnp.float32),
            jax.ShapeDtypeStruct((requests, stacked, HEAD_SIZE), jnp.bfloat16),
        ),
        in_specs=[smem, smem, smem, vmem, vmem, vmem, vmem],
        out_specs=(vmem, vmem, vmem, vmem),
    )
    kept, packed, accum, stacked_q = local_call(
        page_table, cache_len, accepted, parents, queries, tree_rows, pool_slots
    )
    hbm = pl.BlockSpec(memory_space=pl.ANY)
    partial = pl.pallas_call(
        functools.partial(spill_kernel, own_slots),
        out_shape=jax.ShapeDtypeStruct((queries.shape[0], o_weight.shape[1]), jnp.bfloat16),
        in_specs=[smem, smem, hbm, hbm, hbm, hbm, hbm],
        out_specs=vmem,
        scratch_shapes=[
            pltpu.VMEM(packed.shape, packed.dtype),
            pltpu.VMEM(accum.shape, accum.dtype),
            pltpu.VMEM(stacked_q.shape, stacked_q.dtype),
            pltpu.VMEM(spill.shape, spill.dtype),
            pltpu.VMEM(o_weight.shape, o_weight.dtype),
            pltpu.VMEM(queries.shape, jnp.bfloat16),
            pltpu.SemaphoreType.DMA((5,)),
        ],
    )(page_table, cache_len, packed, accum, stacked_q, spill, o_weight)

    parts = lax.axis_size("tp")
    gathered = lax.all_to_all(partial, "tp", 0, 0, tiled=True)
    blocks = gathered.reshape(parts, partial.shape[0] // parts, partial.shape[1])
    summed = blocks[0].astype(jnp.float32)
    for i in range(1, parts):
        summed = summed + blocks[i].astype(jnp.float32)
    projected = summed.astype(jnp.bfloat16)
    return (projected, kept.reshape(kept.shape[0], 1, kept.shape[1]))


def solution(mesh):
    in_specs = (
        P("req", "tp"),
        P("req", "tp", None),
        P("req", "tp", None, None),
        P("req", None),
        P("req"),
        P("req", None),
        P("req"),
        P("tp", None),
    )
    out_specs = (P(("req", "tp"), None), P("req", "tp", None))
    return jax.shard_map(step, mesh=mesh, in_specs=in_specs, out_specs=out_specs, check_vma=False)
```

```python
import functools
import math

import jax
import jax.numpy as jnp
from jax import lax
from jax.experimental import pallas as pl
from jax.experimental.pallas import tpu as pltpu
from jax.sharding import PartitionSpec as P

HEAD_SIZE = 128
LOCAL = 2

very_negative = -1e30


def nt_dot(a, b):
    return lax.dot_general(a, b, (((1,), (1,)), ((), ())), preferred_element_type=jnp.float32)


def stacked_queries(q_ref, rows, heads):
    q = q_ref[rows, :]
    return jnp.concatenate(
        [q[:, g * HEAD_SIZE : (g + 1) * HEAD_SIZE] for g in range(heads)], axis=0
    )


def page_blocks(q_all, pages, first_page, length):
    page_len = pages[0].shape[0]
    keys = jnp.concatenate([page[:, :HEAD_SIZE] for page in pages], axis=0)
    lane = lax.broadcasted_iota(jnp.int32, (1, keys.shape[0]), 1)
    visible = (first_page * page_len + lane) < length
    scores = nt_dot(q_all, keys) * (1.0 / math.sqrt(HEAD_SIZE))
    scores = jnp.where(visible, scores, very_negative)
    blocks = []
    for k, page in enumerate(pages):
        cols = slice(k * page_len, (k + 1) * page_len)
        s = scores[:, cols]
        m = jnp.max(s, axis=1, keepdims=True)
        w = jnp.exp(s - m).astype(jnp.bfloat16)
        l = jnp.sum(w.astype(jnp.float32), axis=1, keepdims=True)
        a = jnp.dot(w, page[:, HEAD_SIZE:], preferred_element_type=jnp.float32)
        blocks.append((m, l, a))
    return blocks


def merge(blocks):
    top = blocks[0][0]
    for m, _, _ in blocks[1:]:
        top = jnp.maximum(top, m)
    total = None
    accum = None
    for m, l, a in blocks:
        f = jnp.exp(m - top)
        total = f * l if total is None else total + f * l
        accum = f * a if accum is None else accum + f * a
    return top, total, accum


def local_kernel(
    table_ref, len_ref, leaf_ref, parents_ref, q_ref, tree_ref, pool_ref,
    kept_ref, ml_ref, a_ref, qs_ref,
):
    n_req, tree_len = parents_ref.shape
    nodes = n_req * tree_len
    heads = q_ref.shape[1] // HEAD_SIZE
    stacked = heads * tree_len
    scale = 1.0 / math.sqrt(HEAD_SIZE)
    sub = lax.broadcasted_iota(jnp.int32, (nodes, nodes), 0)
    lane = lax.broadcasted_iota(jnp.int32, (nodes, nodes), 1)
    eye = (sub == lane).astype(jnp.float32)
    squarings = (tree_len - 1).bit_length()

    parents = parents_ref[...].astype(jnp.float32)
    first = lax.broadcasted_iota(jnp.int32, parents.shape, 0).astype(jnp.float32) * tree_len
    parents = jnp.where(parents >= 0.0, parents + first, -1.0).astype(jnp.bfloat16)
    node = lax.broadcasted_iota(jnp.int32, (tree_len, nodes), 0)
    column = lax.broadcasted_iota(jnp.int32, (tree_len, nodes), 1)
    parent_row = None
    for r in range(n_req):
        place = (column == node + r * tree_len).astype(jnp.bfloat16)
        lhs = jnp.broadcast_to(parents[r : r + 1], (16, tree_len))
        placed = jnp.dot(lhs, place, preferred_element_type=jnp.float32)[0:1]
        parent_row = placed if parent_row is None else parent_row + placed

    rt = eye + (sub.astype(jnp.float32) == parent_row).astype(jnp.float32)
    for _ in range(squarings):
        rb = rt.astype(jnp.bfloat16)
        rt = jnp.minimum(jnp.dot(rb, rb, preferred_element_type=jnp.float32), 1.0)
    reach = nt_dot(eye.astype(jnp.bfloat16), rt.astype(jnp.bfloat16))

    depth = jnp.sum(rt, axis=0, keepdims=True) - 1.0
    slot = lax.broadcasted_iota(jnp.int32, (tree_len, nodes), 0).astype(jnp.float32)
    selectors = []
    for r in range(n_req):
        leaf = r * tree_len + leaf_ref[r]
        kept_mask = jnp.sum(jnp.where(sub == leaf, reach, 0.0), axis=0, keepdims=True)
        selectors.append(jnp.where((slot == depth) & (kept_mask > 0.5), 1.0, 0.0))
    selector = jnp.concatenate(selectors, axis=0).astype(jnp.bfloat16)
    tree_rows = tree_ref[...]
    kept_ref[...] = jnp.dot(selector, tree_rows, preferred_element_type=jnp.float32).astype(
        kept_ref.dtype
    )

    q_all = [stacked_queries(q_ref, pl.ds(r * tree_len, tree_len), heads) for r in range(n_req)]
    for r in range(n_req):
        qs_ref[r] = q_all[r]
    tree_mask = (
        jnp.concatenate(
            [reach[r * tree_len : (r + 1) * tree_len] for r in range(n_req) for _ in range(heads)],
            axis=0,
        )
        > 0.5
    )
    s = nt_dot(jnp.concatenate(q_all, axis=0), tree_rows[:, :HEAD_SIZE]) * scale
    s = jnp.where(tree_mask, s, very_negative)
    m = jnp.max(s, axis=1, keepdims=True)
    w = jnp.exp(s - m).astype(jnp.bfloat16)
    l = jnp.sum(w.astype(jnp.float32), axis=1, keepdims=True)
    a = jnp.dot(w, tree_rows[:, HEAD_SIZE:], preferred_element_type=jnp.float32)

    state_lane = lax.broadcasted_iota(jnp.int32, (stacked, HEAD_SIZE), 1)
    for r in range(n_req):
        rows = slice(r * stacked, (r + 1) * stacked)
        pages = [pool_ref[table_ref[r, k]] for k in range(LOCAL)]
        blocks = [(m[rows], l[rows], a[rows])] + page_blocks(q_all[r], pages, 0, len_ref[r])
        top, total, accum = merge(blocks)
        ml_ref[r] = jnp.where(state_lane == 0, top, jnp.where(state_lane == 1, total, 0.0))
        a_ref[r] = accum


def spill_kernel(
    spill_base, table_ref, len_ref, ml_ref, a_ref, q_ref, spill_ref, weight_hbm,
    proj_ref, weight_vmem, att_sc, m_sc, l_sc, acc_sc, weight_sem,
):
    weight_copy = pltpu.make_async_copy(weight_hbm, weight_vmem, weight_sem)
    weight_copy.start()
    n_req, tree_len = table_ref.shape[0], att_sc.shape[0] // table_ref.shape[0]
    heads = att_sc.shape[1] // HEAD_SIZE
    max_pages = table_ref.shape[1]
    spill_slots = spill_ref.shape[0]
    page_len = spill_ref.shape[1]
    for r in range(n_req):
        rows = pl.ds(r * tree_len, tree_len)
        length = len_ref[r]
        n_pages = (length + page_len - 1) // page_len
        ml = ml_ref[r]
        m_sc[...] = ml[:, 0:1]
        l_sc[...] = ml[:, 1:2]
        acc_sc[...] = a_ref[r]
        for first in range(LOCAL, max_pages, 2):

            @pl.when(first < n_pages)
            def _():
                pages = [
                    spill_ref[jnp.clip(table_ref[r, k] - spill_base, 0, spill_slots - 1)]
                    for k in range(first, min(first + 2, max_pages))
                ]
                state = (m_sc[...], l_sc[...], acc_sc[...])
                top, total, accum = merge([state] + page_blocks(q_ref[r], pages, first, length))
                m_sc[...] = top
                l_sc[...] = total
                acc_sc[...] = accum

        att = (acc_sc[...] / l_sc[...]).astype(att_sc.dtype)
        for g in range(heads):
            att_sc[rows, pl.ds(g * HEAD_SIZE, HEAD_SIZE)] = att[g * tree_len : (g + 1) * tree_len]

    weight_copy.wait()
    proj_ref[...] = jnp.dot(
        att_sc[...], weight_vmem[...], preferred_element_type=jnp.float32
    ).astype(proj_ref.dtype)


def step(queries, tree_kv, page_pool, page_table, cache_len, parents, accepted, o_weight):
    requests, tree_len = parents.shape
    heads = queries.shape[1] // HEAD_SIZE
    pool_slots = page_pool[:, 0]
    own_slots = requests * LOCAL
    ring = lax.axis_size("req")
    spill_source = pool_slots[own_slots:]
    spill = lax.ppermute(spill_source, "req", [((i + 1) % ring, i) for i in range(ring)])
    tree_rows = tree_kv[:, 0, :]
    smem = pl.BlockSpec(memory_space=pltpu.SMEM)
    vmem = pl.BlockSpec(memory_space=pltpu.VMEM)
    stacked = heads * tree_len
    local_call = pl.pallas_call(
        local_kernel,
        out_shape=(
            jax.ShapeDtypeStruct(tree_rows.shape, jnp.bfloat16),
            jax.ShapeDtypeStruct((requests, stacked, HEAD_SIZE), jnp.float32),
            jax.ShapeDtypeStruct((requests, stacked, HEAD_SIZE), jnp.float32),
            jax.ShapeDtypeStruct((requests, stacked, HEAD_SIZE), jnp.bfloat16),
        ),
        in_specs=[smem, smem, smem, vmem, vmem, vmem, vmem],
        out_specs=(vmem, vmem, vmem, vmem),
    )
    kept, packed, accum, stacked_q = local_call(
        page_table, cache_len, accepted, parents, queries, tree_rows, pool_slots
    )
    partial = pl.pallas_call(
        functools.partial(spill_kernel, own_slots),
        out_shape=jax.ShapeDtypeStruct((queries.shape[0], o_weight.shape[1]), jnp.bfloat16),
        in_specs=[smem, smem, vmem, vmem, vmem, vmem, pl.BlockSpec(memory_space=pl.ANY)],
        out_specs=vmem,
        scratch_shapes=[
            pltpu.VMEM(o_weight.shape, o_weight.dtype),
            pltpu.VMEM(queries.shape, jnp.bfloat16),
            pltpu.VMEM((stacked, 1), jnp.float32),
            pltpu.VMEM((stacked, 1), jnp.float32),
            pltpu.VMEM((stacked, HEAD_SIZE), jnp.float32),
            pltpu.SemaphoreType.DMA(()),
        ],
    )(page_table, cache_len, packed, accum, stacked_q, spill, o_weight)

    parts = lax.axis_size("tp")
    gathered = lax.all_to_all(partial, "tp", 0, 0, tiled=True)
    blocks = gathered.reshape(parts, partial.shape[0] // parts, partial.shape[1])
    summed = blocks[0].astype(jnp.float32)
    for i in range(1, parts):
        summed = summed + blocks[i].astype(jnp.float32)
    projected = summed.astype(jnp.bfloat16)
    return (projected, kept.reshape(kept.shape[0], 1, kept.shape[1]))


def solution(mesh):
    in_specs = (
        P("req", "tp"),
        P("req", "tp", None),
        P("req", "tp", None, None),
        P("req", None),
        P("req"),
        P("req", None),
        P("req"),
        P("tp", None),
    )
    out_specs = (P(("req", "tp"), None), P("req", "tp", None))
    return jax.shard_map(step, mesh=mesh, in_specs=in_specs, out_specs=out_specs, check_vma=False)
```

```python
import functools
import math

import jax
import jax.numpy as jnp
from jax import lax
from jax.experimental import pallas as pl
from jax.experimental.pallas import tpu as pltpu
from jax.sharding import PartitionSpec as P

HEAD_SIZE = 128
LOCAL = 2

very_negative = -1e30


def nt_dot(a, b):
    return lax.dot_general(a, b, (((1,), (1,)), ((), ())), preferred_element_type=jnp.float32)


def stacked_queries(q_ref, rows, heads):
    q = q_ref[rows, :]
    return jnp.concatenate(
        [q[:, g * HEAD_SIZE : (g + 1) * HEAD_SIZE] for g in range(heads)], axis=0
    )


def page_blocks(q_all, pages, first_page, length):
    page_len = pages[0].shape[0]
    keys = jnp.concatenate([page[:, :HEAD_SIZE] for page in pages], axis=0)
    lane = lax.broadcasted_iota(jnp.int32, (1, keys.shape[0]), 1)
    visible = (first_page * page_len + lane) < length
    scores = nt_dot(q_all, keys) * (1.0 / math.sqrt(HEAD_SIZE))
    scores = jnp.where(visible, scores, very_negative)
    blocks = []
    for k, page in enumerate(pages):
        cols = slice(k * page_len, (k + 1) * page_len)
        s = scores[:, cols]
        m = jnp.max(s, axis=1, keepdims=True)
        w = jnp.exp(s - m).astype(jnp.bfloat16)
        l = jnp.sum(w.astype(jnp.float32), axis=1, keepdims=True)
        a = jnp.dot(w, page[:, HEAD_SIZE:], preferred_element_type=jnp.float32)
        blocks.append((m, l, a))
    return blocks


def merge(blocks):
    top = blocks[0][0]
    for m, _, _ in blocks[1:]:
        top = jnp.maximum(top, m)
    total = None
    accum = None
    for m, l, a in blocks:
        f = jnp.exp(m - top)
        total = f * l if total is None else total + f * l
        accum = f * a if accum is None else accum + f * a
    return top, total, accum


def local_kernel(
    table_ref, len_ref, leaf_ref, parents_ref, q_ref, tree_ref, pool_ref,
    kept_ref, ml_ref, a_ref, qs_ref,
):
    n_req, tree_len = parents_ref.shape
    nodes = n_req * tree_len
    heads = q_ref.shape[1] // HEAD_SIZE
    stacked = heads * tree_len
    scale = 1.0 / math.sqrt(HEAD_SIZE)
    sub = lax.broadcasted_iota(jnp.int32, (nodes, nodes), 0)
    lane = lax.broadcasted_iota(jnp.int32, (nodes, nodes), 1)
    eye = (sub == lane).astype(jnp.float32)
    squarings = (tree_len - 1).bit_length()

    parents = parents_ref[...].astype(jnp.float32)
    first = lax.broadcasted_iota(jnp.int32, parents.shape, 0).astype(jnp.float32) * tree_len
    parents = jnp.where(parents >= 0.0, parents + first, -1.0).astype(jnp.bfloat16)
    node = lax.broadcasted_iota(jnp.int32, (tree_len, nodes), 0)
    column = lax.broadcasted_iota(jnp.int32, (tree_len, nodes), 1)
    parent_row = None
    for r in range(n_req):
        place = (column == node + r * tree_len).astype(jnp.bfloat16)
        lhs = jnp.broadcast_to(parents[r : r + 1], (16, tree_len))
        placed = jnp.dot(lhs, place, preferred_element_type=jnp.float32)[0:1]
        parent_row = placed if parent_row is None else parent_row + placed

    rt = eye + (sub.astype(jnp.float32) == parent_row).astype(jnp.float32)
    for _ in range(squarings):
        rb = rt.astype(jnp.bfloat16)
        rt = jnp.minimum(jnp.dot(rb, rb, preferred_element_type=jnp.float32), 1.0)
    reach = nt_dot(eye.astype(jnp.bfloat16), rt.astype(jnp.bfloat16))

    depth = jnp.sum(rt, axis=0, keepdims=True) - 1.0
    slot = lax.broadcasted_iota(jnp.int32, (tree_len, nodes), 0).astype(jnp.float32)
    selectors = []
    for r in range(n_req):
        leaf = r * tree_len + leaf_ref[r]
        kept_mask = jnp.sum(jnp.where(sub == leaf, reach, 0.0), axis=0, keepdims=True)
        selectors.append(jnp.where((slot == depth) & (kept_mask > 0.5), 1.0, 0.0))
    selector = jnp.concatenate(selectors, axis=0).astype(jnp.bfloat16)
    tree_rows = tree_ref[...]
    kept_ref[...] = jnp.dot(selector, tree_rows, preferred_element_type=jnp.float32).astype(
        kept_ref.dtype
    )

    q_all = [stacked_queries(q_ref, pl.ds(r * tree_len, tree_len), heads) for r in range(n_req)]
    for r in range(n_req):
        qs_ref[r] = q_all[r]
    tree_mask = (
        jnp.concatenate(
            [reach[r * tree_len : (r + 1) * tree_len] for r in range(n_req) for _ in range(heads)],
            axis=0,
        )
        > 0.5
    )
    s = nt_dot(jnp.concatenate(q_all, axis=0), tree_rows[:, :HEAD_SIZE]) * scale
    s = jnp.where(tree_mask, s, very_negative)
    m = jnp.max(s, axis=1, keepdims=True)
    w = jnp.exp(s - m).astype(jnp.bfloat16)
    l = jnp.sum(w.astype(jnp.float32), axis=1, keepdims=True)
    a = jnp.dot(w, tree_rows[:, HEAD_SIZE:], preferred_element_type=jnp.float32)

    state_lane = lax.broadcasted_iota(jnp.int32, (stacked, HEAD_SIZE), 1)
    for r in range(n_req):
        rows = slice(r * stacked, (r + 1) * stacked)
        pages = [pool_ref[table_ref[r, k]] for k in range(LOCAL)]
        blocks = [(m[rows], l[rows], a[rows])] + page_blocks(q_all[r], pages, 0, len_ref[r])
        top, total, accum = merge(blocks)
        ml_ref[r] = jnp.where(state_lane == 0, top, jnp.where(state_lane == 1, total, 0.0))
        a_ref[r] = accum


def spill_kernel(
    spill_base, table_ref, len_ref, ml_ref, a_ref, q_ref, spill_ref, weight_hbm,
    proj_ref, weight_vmem, att_sc, owner_sc, page_sc, weight_sem,
):
    weight_copy = pltpu.make_async_copy(weight_hbm, weight_vmem, weight_sem)
    weight_copy.start()
    n_req, tree_len = table_ref.shape[0], att_sc.shape[0] // table_ref.shape[0]
    heads = att_sc.shape[1] // HEAD_SIZE
    max_pages = table_ref.shape[1]
    spill_slots, page_len = spill_ref.shape[0], spill_ref.shape[1]
    scale = 1.0 / math.sqrt(HEAD_SIZE)

    for slot in range(spill_slots):
        owner_sc[slot] = 0
        page_sc[slot] = max_pages
    for r in range(n_req):
        n_pages = (len_ref[r] + page_len - 1) // page_len
        for k in range(LOCAL, max_pages):

            @pl.when(k < n_pages)
            def _():
                slot = jnp.clip(table_ref[r, k] - spill_base, 0, spill_slots - 1)
                owner_sc[slot] = r
                page_sc[slot] = k

    lane = lax.broadcasted_iota(jnp.int32, (1, page_len), 1)
    blocks = []
    for slot in range(spill_slots):
        owner = owner_sc[slot]
        visible = (page_sc[slot] * page_len + lane) < len_ref[owner]
        page = spill_ref[slot]
        scores = nt_dot(q_ref[owner], page[:, :HEAD_SIZE]) * scale
        scores = jnp.where(visible, scores, very_negative)
        m = jnp.max(scores, axis=1, keepdims=True)
        w = jnp.exp(scores - m).astype(jnp.bfloat16)
        l = jnp.sum(w.astype(jnp.float32), axis=1, keepdims=True)
        a = jnp.dot(w, page[:, HEAD_SIZE:], preferred_element_type=jnp.float32)
        blocks.append((owner, m, l, a))

    for r in range(n_req):
        rows = pl.ds(r * tree_len, tree_len)
        ml = ml_ref[r]
        state = (ml[:, 0:1], ml[:, 1:2], a_ref[r])
        mine = [(jnp.where(owner == r, m, very_negative), l, a) for owner, m, l, a in blocks]
        _, total, accum = merge([state] + mine)
        att = (accum / total).astype(att_sc.dtype)
        for g in range(heads):
            att_sc[rows, pl.ds(g * HEAD_SIZE, HEAD_SIZE)] = att[g * tree_len : (g + 1) * tree_len]

    weight_copy.wait()
    proj_ref[...] = jnp.dot(
        att_sc[...], weight_vmem[...], preferred_element_type=jnp.float32
    ).astype(proj_ref.dtype)


def step(queries, tree_kv, page_pool, page_table, cache_len, parents, accepted, o_weight):
    requests, tree_len = parents.shape
    heads = queries.shape[1] // HEAD_SIZE
    pool_slots = page_pool[:, 0]
    own_slots = requests * LOCAL
    ring = lax.axis_size("req")
    spill_source = pool_slots[own_slots:]
    spill = lax.ppermute(spill_source, "req", [((i + 1) % ring, i) for i in range(ring)])
    tree_rows = tree_kv[:, 0, :]
    smem = pl.BlockSpec(memory_space=pltpu.SMEM)
    vmem = pl.BlockSpec(memory_space=pltpu.VMEM)
    stacked = heads * tree_len
    local_call = pl.pallas_call(
        local_kernel,
        out_shape=(
            jax.ShapeDtypeStruct(tree_rows.shape, jnp.bfloat16),
            jax.ShapeDtypeStruct((requests, stacked, HEAD_SIZE), jnp.float32),
            jax.ShapeDtypeStruct((requests, stacked, HEAD_SIZE), jnp.float32),
            jax.ShapeDtypeStruct((requests, stacked, HEAD_SIZE), jnp.bfloat16),
        ),
        in_specs=[smem, smem, smem, vmem, vmem, vmem, vmem],
        out_specs=(vmem, vmem, vmem, vmem),
    )
    kept, packed, accum, stacked_q = local_call(
        page_table, cache_len, accepted, parents, queries, tree_rows, pool_slots
    )
    partial = pl.pallas_call(
        functools.partial(spill_kernel, own_slots),
        out_shape=jax.ShapeDtypeStruct((queries.shape[0], o_weight.shape[1]), jnp.bfloat16),
        in_specs=[smem, smem, vmem, vmem, vmem, vmem, pl.BlockSpec(memory_space=pl.ANY)],
        out_specs=vmem,
        scratch_shapes=[
            pltpu.VMEM(o_weight.shape, o_weight.dtype),
            pltpu.VMEM(queries.shape, jnp.bfloat16),
            pltpu.SMEM((spill.shape[0],), jnp.int32),
            pltpu.SMEM((spill.shape[0],), jnp.int32),
            pltpu.SemaphoreType.DMA(()),
        ],
    )(page_table, cache_len, packed, accum, stacked_q, spill, o_weight)

    parts = lax.axis_size("tp")
    gathered = lax.all_to_all(partial, "tp", 0, 0, tiled=True)
    blocks = gathered.reshape(parts, partial.shape[0] // parts, partial.shape[1])
    summed = blocks[0].astype(jnp.float32)
    for i in range(1, parts):
        summed = summed + blocks[i].astype(jnp.float32)
    projected = summed.astype(jnp.bfloat16)
    return (projected, kept.reshape(kept.shape[0], 1, kept.shape[1]))


def solution(mesh):
    in_specs = (
        P("req", "tp"),
        P("req", "tp", None),
        P("req", "tp", None, None),
        P("req", None),
        P("req"),
        P("req", None),
        P("req"),
        P("tp", None),
    )
    out_specs = (P(("req", "tp"), None), P("req", "tp", None))
    return jax.shard_map(step, mesh=mesh, in_specs=in_specs, out_specs=out_specs, check_vma=False)
```

```python
import functools
import math

import jax
import jax.numpy as jnp
from jax import lax
from jax.experimental import pallas as pl
from jax.experimental.pallas import tpu as pltpu
from jax.sharding import PartitionSpec as P

HEAD_SIZE = 128
LOCAL = 2

very_negative = -1e30


def nt_dot(a, b):
    return lax.dot_general(a, b, (((1,), (1,)), ((), ())), preferred_element_type=jnp.float32)


def stacked_queries(q_ref, rows, heads):
    q = q_ref[rows, :]
    return jnp.concatenate(
        [q[:, g * HEAD_SIZE : (g + 1) * HEAD_SIZE] for g in range(heads)], axis=0
    )


def page_blocks(q_all, pages, first_page, length):
    page_len = pages[0].shape[0]
    keys = jnp.concatenate([page[:, :HEAD_SIZE] for page in pages], axis=0)
    lane = lax.broadcasted_iota(jnp.int32, (1, keys.shape[0]), 1)
    visible = (first_page * page_len + lane) < length
    scores = nt_dot(q_all, keys) * (1.0 / math.sqrt(HEAD_SIZE))
    scores = jnp.where(visible, scores, very_negative)
    blocks = []
    for k, page in enumerate(pages):
        cols = slice(k * page_len, (k + 1) * page_len)
        s = scores[:, cols]
        m = jnp.max(s, axis=1, keepdims=True)
        w = jnp.exp(s - m).astype(jnp.bfloat16)
        l = jnp.sum(w.astype(jnp.float32), axis=1, keepdims=True)
        a = jnp.dot(w, page[:, HEAD_SIZE:], preferred_element_type=jnp.float32)
        blocks.append((m, l, a))
    return blocks


def merge(blocks):
    top = blocks[0][0]
    for m, _, _ in blocks[1:]:
        top = jnp.maximum(top, m)
    total = None
    accum = None
    for m, l, a in blocks:
        f = jnp.exp(m - top)
        total = f * l if total is None else total + f * l
        accum = f * a if accum is None else accum + f * a
    return top, total, accum


def local_kernel(
    table_ref, len_ref, leaf_ref, parents_ref, q_ref, tree_ref, pool_ref,
    kept_ref, ml_ref, a_ref, qs_ref,
):
    n_req, tree_len = parents_ref.shape
    nodes = n_req * tree_len
    heads = q_ref.shape[1] // HEAD_SIZE
    stacked = heads * tree_len
    scale = 1.0 / math.sqrt(HEAD_SIZE)
    sub = lax.broadcasted_iota(jnp.int32, (nodes, nodes), 0)
    lane = lax.broadcasted_iota(jnp.int32, (nodes, nodes), 1)
    eye = (sub == lane).astype(jnp.float32)
    squarings = (tree_len - 1).bit_length()

    parents = parents_ref[...].astype(jnp.float32)
    first = lax.broadcasted_iota(jnp.int32, parents.shape, 0).astype(jnp.float32) * tree_len
    parents = jnp.where(parents >= 0.0, parents + first, -1.0).astype(jnp.bfloat16)
    node = lax.broadcasted_iota(jnp.int32, (tree_len, nodes), 0)
    column = lax.broadcasted_iota(jnp.int32, (tree_len, nodes), 1)
    parent_row = None
    for r in range(n_req):
        place = (column == node + r * tree_len).astype(jnp.bfloat16)
        lhs = jnp.broadcast_to(parents[r : r + 1], (16, tree_len))
        placed = jnp.dot(lhs, place, preferred_element_type=jnp.float32)[0:1]
        parent_row = placed if parent_row is None else parent_row + placed

    rt = eye + (sub.astype(jnp.float32) == parent_row).astype(jnp.float32)
    for _ in range(squarings):
        rb = rt.astype(jnp.bfloat16)
        rt = jnp.minimum(jnp.dot(rb, rb, preferred_element_type=jnp.float32), 1.0)
    reach = nt_dot(eye.astype(jnp.bfloat16), rt.astype(jnp.bfloat16))

    depth = jnp.sum(rt, axis=0, keepdims=True) - 1.0
    slot = lax.broadcasted_iota(jnp.int32, (tree_len, nodes), 0).astype(jnp.float32)
    selectors = []
    for r in range(n_req):
        leaf = r * tree_len + leaf_ref[r]
        kept_mask = jnp.sum(jnp.where(sub == leaf, reach, 0.0), axis=0, keepdims=True)
        selectors.append(jnp.where((slot == depth) & (kept_mask > 0.5), 1.0, 0.0))
    selector = jnp.concatenate(selectors, axis=0).astype(jnp.bfloat16)
    tree_rows = tree_ref[...]
    kept_ref[...] = jnp.dot(selector, tree_rows, preferred_element_type=jnp.float32).astype(
        kept_ref.dtype
    )

    q_all = [stacked_queries(q_ref, pl.ds(r * tree_len, tree_len), heads) for r in range(n_req)]
    for r in range(n_req):
        qs_ref[r] = q_all[r]
    tree_mask = (
        jnp.concatenate(
            [reach[r * tree_len : (r + 1) * tree_len] for r in range(n_req) for _ in range(heads)],
            axis=0,
        )
        > 0.5
    )
    s = nt_dot(jnp.concatenate(q_all, axis=0), tree_rows[:, :HEAD_SIZE]) * scale
    s = jnp.where(tree_mask, s, very_negative)
    m = jnp.max(s, axis=1, keepdims=True)
    w = jnp.exp(s - m).astype(jnp.bfloat16)
    l = jnp.sum(w.astype(jnp.float32), axis=1, keepdims=True)
    a = jnp.dot(w, tree_rows[:, HEAD_SIZE:], preferred_element_type=jnp.float32)

    state_lane = lax.broadcasted_iota(jnp.int32, (stacked, HEAD_SIZE), 1)
    for r in range(n_req):
        rows = slice(r * stacked, (r + 1) * stacked)
        pages = [pool_ref[table_ref[r, k]] for k in range(LOCAL)]
        blocks = [(m[rows], l[rows], a[rows])] + page_blocks(q_all[r], pages, 0, len_ref[r])
        top, total, accum = merge(blocks)
        ml_ref[r] = jnp.where(state_lane == 0, top, jnp.where(state_lane == 1, total, 0.0))
        a_ref[r] = accum


def spill_kernel(
    spill_base, table_ref, len_ref, tp_ref, ml_ref, a_ref, q_ref, spill_ref, weight_hbm,
    proj0_ref, proj1_ref, proj2_ref, proj3_ref, weight_vmem, att_sc, proj_sc, weight_sem,
):
    weight_copy = pltpu.make_async_copy(weight_hbm, weight_vmem, weight_sem)
    weight_copy.start()
    n_req, tree_len = table_ref.shape[0], att_sc.shape[0] // table_ref.shape[0]
    heads = att_sc.shape[1] // HEAD_SIZE
    max_pages = table_ref.shape[1]
    spill_slots = spill_ref.shape[0]
    for r in range(n_req):
        rows = pl.ds(r * tree_len, tree_len)
        q_all = q_ref[r]
        pages = [
            spill_ref[jnp.clip(table_ref[r, k] - spill_base, 0, spill_slots - 1)]
            for k in range(LOCAL, max_pages)
        ]
        ml = ml_ref[r]
        state = (ml[:, 0:1], ml[:, 1:2], a_ref[r])
        _, total, accum = merge([state] + page_blocks(q_all, pages, LOCAL, len_ref[r]))
        att = (accum / total).astype(att_sc.dtype)
        for g in range(heads):
            att_sc[rows, pl.ds(g * HEAD_SIZE, HEAD_SIZE)] = att[g * tree_len : (g + 1) * tree_len]

    weight_copy.wait()
    proj_sc[...] = jnp.dot(
        att_sc[...], weight_vmem[...], preferred_element_type=jnp.float32
    ).astype(proj_sc.dtype)
    outs = (proj0_ref, proj1_ref, proj2_ref, proj3_ref)
    block = outs[0].shape[0]
    for j, out in enumerate(outs):
        start = pl.multiple_of(((tp_ref[0] + j) % len(outs)) * block, block)
        out[...] = proj_sc[pl.ds(start, block), :]


def step(queries, tree_kv, page_pool, page_table, cache_len, parents, accepted, o_weight):
    requests, tree_len = parents.shape
    heads = queries.shape[1] // HEAD_SIZE
    pool_slots = page_pool[:, 0]
    own_slots = requests * LOCAL
    ring = lax.axis_size("req")
    spill_source = pool_slots[own_slots:]
    spill = lax.ppermute(spill_source, "req", [((i + 1) % ring, i) for i in range(ring)])
    tree_rows = tree_kv[:, 0, :]
    smem = pl.BlockSpec(memory_space=pltpu.SMEM)
    vmem = pl.BlockSpec(memory_space=pltpu.VMEM)
    stacked = heads * tree_len
    local_call = pl.pallas_call(
        local_kernel,
        out_shape=(
            jax.ShapeDtypeStruct(tree_rows.shape, jnp.bfloat16),
            jax.ShapeDtypeStruct((requests, stacked, HEAD_SIZE), jnp.float32),
            jax.ShapeDtypeStruct((requests, stacked, HEAD_SIZE), jnp.float32),
            jax.ShapeDtypeStruct((requests, stacked, HEAD_SIZE), jnp.bfloat16),
        ),
        in_specs=[smem, smem, smem, vmem, vmem, vmem, vmem],
        out_specs=(vmem, vmem, vmem, vmem),
    )
    kept, packed, accum, stacked_q = local_call(
        page_table, cache_len, accepted, parents, queries, tree_rows, pool_slots
    )
    parts = lax.axis_size("tp")
    me = lax.axis_index("tp")
    block_rows = queries.shape[0] // parts
    rotated = pl.pallas_call(
        functools.partial(spill_kernel, own_slots),
        out_shape=tuple(
            jax.ShapeDtypeStruct((block_rows, o_weight.shape[1]), jnp.bfloat16) for _ in range(parts)
        ),
        in_specs=[smem, smem, smem, vmem, vmem, vmem, vmem, pl.BlockSpec(memory_space=pl.ANY)],
        out_specs=tuple(vmem for _ in range(parts)),
        scratch_shapes=[
            pltpu.VMEM(o_weight.shape, o_weight.dtype),
            pltpu.VMEM(queries.shape, jnp.bfloat16),
            pltpu.VMEM((queries.shape[0], o_weight.shape[1]), jnp.bfloat16),
            pltpu.SemaphoreType.DMA(()),
        ],
    )(page_table, cache_len, me.astype(jnp.int32).reshape(1), packed, accum, stacked_q, spill, o_weight)

    summed = rotated[0].astype(jnp.float32)
    for shift in range(1, parts):
        route = [(i, (i + shift) % parts) for i in range(parts)]
        summed = summed + lax.ppermute(rotated[shift], "tp", route).astype(jnp.float32)
    projected = summed.astype(jnp.bfloat16)
    return (projected, kept.reshape(kept.shape[0], 1, kept.shape[1]))


def solution(mesh):
    in_specs = (
        P("req", "tp"),
        P("req", "tp", None),
        P("req", "tp", None, None),
        P("req", None),
        P("req"),
        P("req", None),
        P("req"),
        P("tp", None),
    )
    out_specs = (P(("req", "tp"), None), P("req", "tp", None))
    return jax.shard_map(step, mesh=mesh, in_specs=in_specs, out_specs=out_specs, check_vma=False)
```

```python
import functools
import math

import jax
import jax.numpy as jnp
from jax import lax
from jax.experimental import pallas as pl
from jax.experimental.pallas import tpu as pltpu
from jax.sharding import PartitionSpec as P

HEAD_SIZE = 128
LOCAL = 2

very_negative = -1e30


def nt_dot(a, b):
    return lax.dot_general(a, b, (((1,), (1,)), ((), ())), preferred_element_type=jnp.float32)


def stacked_queries(q_ref, rows, heads):
    q = q_ref[rows, :]
    return jnp.concatenate(
        [q[:, g * HEAD_SIZE : (g + 1) * HEAD_SIZE] for g in range(heads)], axis=0
    )


def page_blocks(q_all, pages, first_page, length):
    page_len = pages[0].shape[0]
    keys = jnp.concatenate([page[:, :HEAD_SIZE] for page in pages], axis=0)
    lane = lax.broadcasted_iota(jnp.int32, (1, keys.shape[0]), 1)
    visible = (first_page * page_len + lane) < length
    scores = nt_dot(q_all, keys) * (1.0 / math.sqrt(HEAD_SIZE))
    scores = jnp.where(visible, scores, very_negative)
    blocks = []
    for k, page in enumerate(pages):
        cols = slice(k * page_len, (k + 1) * page_len)
        s = scores[:, cols]
        m = jnp.max(s, axis=1, keepdims=True)
        w = jnp.exp(s - m).astype(jnp.bfloat16)
        l = jnp.sum(w.astype(jnp.float32), axis=1, keepdims=True)
        a = jnp.dot(w, page[:, HEAD_SIZE:], preferred_element_type=jnp.float32)
        blocks.append((m, l, a))
    return blocks


def merge(blocks):
    top = blocks[0][0]
    for m, _, _ in blocks[1:]:
        top = jnp.maximum(top, m)
    total = None
    accum = None
    for m, l, a in blocks:
        f = jnp.exp(m - top)
        total = f * l if total is None else total + f * l
        accum = f * a if accum is None else accum + f * a
    return top, total, accum


def local_kernel(
    table_ref, len_ref, leaf_ref, parents_ref, q_ref, tree_ref, pool_ref,
    kept_ref, ml_ref, a_ref, qs_ref,
):
    n_req, tree_len = parents_ref.shape
    nodes = n_req * tree_len
    heads = q_ref.shape[1] // HEAD_SIZE
    stacked = heads * tree_len
    scale = 1.0 / math.sqrt(HEAD_SIZE)
    sub = lax.broadcasted_iota(jnp.int32, (nodes, nodes), 0)
    lane = lax.broadcasted_iota(jnp.int32, (nodes, nodes), 1)
    eye = (sub == lane).astype(jnp.float32)
    squarings = (tree_len - 1).bit_length()

    parents = parents_ref[...].astype(jnp.float32)
    first = lax.broadcasted_iota(jnp.int32, parents.shape, 0).astype(jnp.float32) * tree_len
    parents = jnp.where(parents >= 0.0, parents + first, -1.0).astype(jnp.bfloat16)
    node = lax.broadcasted_iota(jnp.int32, (tree_len, nodes), 0)
    column = lax.broadcasted_iota(jnp.int32, (tree_len, nodes), 1)
    parent_row = None
    for r in range(n_req):
        place = (column == node + r * tree_len).astype(jnp.bfloat16)
        lhs = jnp.broadcast_to(parents[r : r + 1], (16, tree_len))
        placed = jnp.dot(lhs, place, preferred_element_type=jnp.float32)[0:1]
        parent_row = placed if parent_row is None else parent_row + placed

    rt = eye + (sub.astype(jnp.float32) == parent_row).astype(jnp.float32)
    for _ in range(squarings):
        rb = rt.astype(jnp.bfloat16)
        rt = jnp.minimum(jnp.dot(rb, rb, preferred_element_type=jnp.float32), 1.0)
    reach = nt_dot(eye.astype(jnp.bfloat16), rt.astype(jnp.bfloat16))

    depth = jnp.sum(rt, axis=0, keepdims=True) - 1.0
    slot = lax.broadcasted_iota(jnp.int32, (tree_len, nodes), 0).astype(jnp.float32)
    selectors = []
    for r in range(n_req):
        leaf = r * tree_len + leaf_ref[r]
        kept_mask = jnp.sum(jnp.where(sub == leaf, reach, 0.0), axis=0, keepdims=True)
        selectors.append(jnp.where((slot == depth) & (kept_mask > 0.5), 1.0, 0.0))
    selector = jnp.concatenate(selectors, axis=0).astype(jnp.bfloat16)
    tree_rows = tree_ref[...]
    kept_ref[...] = jnp.dot(selector, tree_rows, preferred_element_type=jnp.float32).astype(
        kept_ref.dtype
    )

    q_all = [stacked_queries(q_ref, pl.ds(r * tree_len, tree_len), heads) for r in range(n_req)]
    for r in range(n_req):
        qs_ref[r] = q_all[r]
    tree_mask = (
        jnp.concatenate(
            [reach[r * tree_len : (r + 1) * tree_len] for r in range(n_req) for _ in range(heads)],
            axis=0,
        )
        > 0.5
    )
    s = nt_dot(jnp.concatenate(q_all, axis=0), tree_rows[:, :HEAD_SIZE]) * scale
    s = jnp.where(tree_mask, s, very_negative)
    m = jnp.max(s, axis=1, keepdims=True)
    w = jnp.exp(s - m).astype(jnp.bfloat16)
    l = jnp.sum(w.astype(jnp.float32), axis=1, keepdims=True)
    a = jnp.dot(w, tree_rows[:, HEAD_SIZE:], preferred_element_type=jnp.float32)

    state_lane = lax.broadcasted_iota(jnp.int32, (stacked, HEAD_SIZE), 1)
    for r in range(n_req):
        rows = slice(r * stacked, (r + 1) * stacked)
        pages = [pool_ref[table_ref[r, k]] for k in range(LOCAL)]
        blocks = [(m[rows], l[rows], a[rows])] + page_blocks(q_all[r], pages, 0, len_ref[r])
        top, total, accum = merge(blocks)
        ml_ref[r] = jnp.where(state_lane == 0, top, jnp.where(state_lane == 1, total, 0.0))
        a_ref[r] = accum


def spill_kernel(
    spill_base, table_ref, len_ref, ml_ref, a_ref, q_ref, spill_ref, weight_hbm,
    proj_ref, weight_vmem, att_sc, weight_sem,
):
    weight_rows = weight_vmem.shape[0] // HEAD_SIZE
    weight_copies = [
        pltpu.make_async_copy(
            weight_hbm.at[pl.ds(g * HEAD_SIZE, HEAD_SIZE)],
            weight_vmem.at[pl.ds(g * HEAD_SIZE, HEAD_SIZE)],
            weight_sem.at[g],
        )
        for g in range(weight_rows)
    ]
    for copy in weight_copies:
        copy.start()
    n_req, tree_len = table_ref.shape[0], att_sc.shape[0] // table_ref.shape[0]
    heads = att_sc.shape[1] // HEAD_SIZE
    max_pages = table_ref.shape[1]
    spill_slots = spill_ref.shape[0]
    for r in range(n_req):
        rows = pl.ds(r * tree_len, tree_len)
        q_all = q_ref[r]
        pages = [
            spill_ref[jnp.clip(table_ref[r, k] - spill_base, 0, spill_slots - 1)]
            for k in range(LOCAL, max_pages)
        ]
        ml = ml_ref[r]
        state = (ml[:, 0:1], ml[:, 1:2], a_ref[r])
        _, total, accum = merge([state] + page_blocks(q_all, pages, LOCAL, len_ref[r]))
        att = (accum / total).astype(att_sc.dtype)
        for g in range(heads):
            att_sc[rows, pl.ds(g * HEAD_SIZE, HEAD_SIZE)] = att[g * tree_len : (g + 1) * tree_len]

    proj = None
    for g, copy in enumerate(weight_copies):
        copy.wait()
        rows = pl.ds(g * HEAD_SIZE, HEAD_SIZE)
        part = jnp.dot(att_sc[:, rows], weight_vmem[rows, :], preferred_element_type=jnp.float32)
        proj = part if proj is None else proj + part
    proj_ref[...] = proj.astype(proj_ref.dtype)


def step(queries, tree_kv, page_pool, page_table, cache_len, parents, accepted, o_weight):
    requests, tree_len = parents.shape
    heads = queries.shape[1] // HEAD_SIZE
    pool_slots = page_pool[:, 0]
    own_slots = requests * LOCAL
    ring = lax.axis_size("req")
    spill_source = pool_slots[own_slots:]
    spill = lax.ppermute(spill_source, "req", [((i + 1) % ring, i) for i in range(ring)])
    tree_rows = tree_kv[:, 0, :]
    smem = pl.BlockSpec(memory_space=pltpu.SMEM)
    vmem = pl.BlockSpec(memory_space=pltpu.VMEM)
    stacked = heads * tree_len
    local_call = pl.pallas_call(
        local_kernel,
        out_shape=(
            jax.ShapeDtypeStruct(tree_rows.shape, jnp.bfloat16),
            jax.ShapeDtypeStruct((requests, stacked, HEAD_SIZE), jnp.float32),
            jax.ShapeDtypeStruct((requests, stacked, HEAD_SIZE), jnp.float32),
            jax.ShapeDtypeStruct((requests, stacked, HEAD_SIZE), jnp.bfloat16),
        ),
        in_specs=[smem, smem, smem, vmem, vmem, vmem, vmem],
        out_specs=(vmem, vmem, vmem, vmem),
    )
    kept, packed, accum, stacked_q = local_call(
        page_table, cache_len, accepted, parents, queries, tree_rows, pool_slots
    )
    partial = pl.pallas_call(
        functools.partial(spill_kernel, own_slots),
        out_shape=jax.ShapeDtypeStruct((queries.shape[0], o_weight.shape[1]), jnp.bfloat16),
        in_specs=[smem, smem, vmem, vmem, vmem, vmem, pl.BlockSpec(memory_space=pl.ANY)],
        out_specs=vmem,
        scratch_shapes=[
            pltpu.VMEM(o_weight.shape, o_weight.dtype),
            pltpu.VMEM(queries.shape, jnp.bfloat16),
            pltpu.SemaphoreType.DMA((heads,)),
        ],
    )(page_table, cache_len, packed, accum, stacked_q, spill, o_weight)

    parts = lax.axis_size("tp")
    gathered = lax.all_to_all(partial, "tp", 0, 0, tiled=True)
    blocks = gathered.reshape(parts, partial.shape[0] // parts, partial.shape[1])
    summed = blocks[0].astype(jnp.float32)
    for i in range(1, parts):
        summed = summed + blocks[i].astype(jnp.float32)
    projected = summed.astype(jnp.bfloat16)
    return (projected, kept.reshape(kept.shape[0], 1, kept.shape[1]))


def solution(mesh):
    in_specs = (
        P("req", "tp"),
        P("req", "tp", None),
        P("req", "tp", None, None),
        P("req", None),
        P("req"),
        P("req", None),
        P("req"),
        P("tp", None),
    )
    out_specs = (P(("req", "tp"), None), P("req", "tp", None))
    return jax.shard_map(step, mesh=mesh, in_specs=in_specs, out_specs=out_specs, check_vma=False)
```

```python
import functools
import math

import jax
import jax.numpy as jnp
from jax import lax
from jax.experimental import pallas as pl
from jax.experimental.pallas import tpu as pltpu
from jax.sharding import PartitionSpec as P

HEAD_SIZE = 128
LOCAL = 2

very_negative = -1e30


def nt_dot(a, b):
    return lax.dot_general(a, b, (((1,), (1,)), ((), ())), preferred_element_type=jnp.float32)


def stacked_queries(q_ref, rows, heads):
    q = q_ref[rows, :]
    return jnp.concatenate(
        [q[:, g * HEAD_SIZE : (g + 1) * HEAD_SIZE] for g in range(heads)], axis=0
    )


def page_blocks(q_all, pages, first_page, length):
    page_len = pages[0].shape[0]
    keys = jnp.concatenate([page[:, :HEAD_SIZE] for page in pages], axis=0)
    lane = lax.broadcasted_iota(jnp.int32, (1, keys.shape[0]), 1)
    visible = (first_page * page_len + lane) < length
    scores = nt_dot(q_all, keys) * (1.0 / math.sqrt(HEAD_SIZE))
    scores = jnp.where(visible, scores, very_negative)
    blocks = []
    for k, page in enumerate(pages):
        cols = slice(k * page_len, (k + 1) * page_len)
        s = scores[:, cols]
        m = jnp.max(s, axis=1, keepdims=True)
        w = jnp.exp(s - m).astype(jnp.bfloat16)
        l = jnp.sum(w.astype(jnp.float32), axis=1, keepdims=True)
        a = jnp.dot(w, page[:, HEAD_SIZE:], preferred_element_type=jnp.float32)
        blocks.append((m, l, a))
    return blocks


def merge(blocks):
    top = blocks[0][0]
    for m, _, _ in blocks[1:]:
        top = jnp.maximum(top, m)
    total = None
    accum = None
    for m, l, a in blocks:
        f = jnp.exp(m - top)
        total = f * l if total is None else total + f * l
        accum = f * a if accum is None else accum + f * a
    return top, total, accum


def local_kernel(
    table_ref, len_ref, leaf_ref, parents_ref, q_ref, tree_ref, pool_ref,
    kept_ref, ml_ref, a_ref, qs_ref,
):
    n_req, tree_len = parents_ref.shape
    nodes = n_req * tree_len
    heads = q_ref.shape[1] // HEAD_SIZE
    stacked = heads * tree_len
    scale = 1.0 / math.sqrt(HEAD_SIZE)
    sub = lax.broadcasted_iota(jnp.int32, (nodes, nodes), 0)
    lane = lax.broadcasted_iota(jnp.int32, (nodes, nodes), 1)
    eye = (sub == lane).astype(jnp.float32)
    squarings = (tree_len - 1).bit_length()

    parents = parents_ref[...].astype(jnp.float32)
    first = lax.broadcasted_iota(jnp.int32, parents.shape, 0).astype(jnp.float32) * tree_len
    parents = jnp.where(parents >= 0.0, parents + first, -1.0).astype(jnp.bfloat16)
    node = lax.broadcasted_iota(jnp.int32, (tree_len, nodes), 0)
    column = lax.broadcasted_iota(jnp.int32, (tree_len, nodes), 1)
    parent_row = None
    for r in range(n_req):
        place = (column == node + r * tree_len).astype(jnp.bfloat16)
        lhs = jnp.broadcast_to(parents[r : r + 1], (16, tree_len))
        placed = jnp.dot(lhs, place, preferred_element_type=jnp.float32)[0:1]
        parent_row = placed if parent_row is None else parent_row + placed

    rt = eye + (sub.astype(jnp.float32) == parent_row).astype(jnp.float32)
    for _ in range(squarings):
        rb = rt.astype(jnp.bfloat16)
        rt = jnp.minimum(jnp.dot(rb, rb, preferred_element_type=jnp.float32), 1.0)
    reach = nt_dot(eye.astype(jnp.bfloat16), rt.astype(jnp.bfloat16))

    depth = jnp.sum(rt, axis=0, keepdims=True) - 1.0
    slot = lax.broadcasted_iota(jnp.int32, (tree_len, nodes), 0).astype(jnp.float32)
    selectors = []
    for r in range(n_req):
        leaf = r * tree_len + leaf_ref[r]
        kept_mask = jnp.sum(jnp.where(sub == leaf, reach, 0.0), axis=0, keepdims=True)
        selectors.append(jnp.where((slot == depth) & (kept_mask > 0.5), 1.0, 0.0))
    selector = jnp.concatenate(selectors, axis=0).astype(jnp.bfloat16)
    tree_rows = tree_ref[...]
    kept_ref[...] = jnp.dot(selector, tree_rows, preferred_element_type=jnp.float32).astype(
        kept_ref.dtype
    )

    q_all = [stacked_queries(q_ref, pl.ds(r * tree_len, tree_len), heads) for r in range(n_req)]
    for r in range(n_req):
        qs_ref[r] = q_all[r]
    tree_mask = (
        jnp.concatenate(
            [reach[r * tree_len : (r + 1) * tree_len] for r in range(n_req) for _ in range(heads)],
            axis=0,
        )
        > 0.5
    )
    s = nt_dot(jnp.concatenate(q_all, axis=0), tree_rows[:, :HEAD_SIZE]) * scale
    s = jnp.where(tree_mask, s, very_negative)
    m = jnp.max(s, axis=1, keepdims=True)
    w = jnp.exp(s - m).astype(jnp.bfloat16)
    l = jnp.sum(w.astype(jnp.float32), axis=1, keepdims=True)
    a = jnp.dot(w, tree_rows[:, HEAD_SIZE:], preferred_element_type=jnp.float32)

    state_lane = lax.broadcasted_iota(jnp.int32, (stacked, HEAD_SIZE), 1)
    for r in range(n_req):
        rows = slice(r * stacked, (r + 1) * stacked)
        pages = [pool_ref[table_ref[r, k]] for k in range(LOCAL)]
        blocks = [(m[rows], l[rows], a[rows])] + page_blocks(q_all[r], pages, 0, len_ref[r])
        top, total, accum = merge(blocks)
        ml_ref[r] = jnp.where(state_lane == 0, top, jnp.where(state_lane == 1, total, 0.0))
        a_ref[r] = accum


def spill_kernel(
    spill_base, table_ref, len_ref, ml_ref, a_ref, q_ref, spill_ref, weight_hbm,
    proj_ref, weight_vmem, att_sc, weight_sem,
):
    weight_copy = pltpu.make_async_copy(weight_hbm, weight_vmem, weight_sem)
    weight_copy.start()
    n_req, tree_len = table_ref.shape[0], att_sc.shape[0] // table_ref.shape[0]
    heads = att_sc.shape[1] // HEAD_SIZE
    max_pages = table_ref.shape[1]
    spill_slots = spill_ref.shape[0]
    for r in range(n_req):
        rows = pl.ds(r * tree_len, tree_len)
        q_all = q_ref[r]
        pages = [
            spill_ref[jnp.clip(table_ref[r, k] - spill_base, 0, spill_slots - 1)]
            for k in range(LOCAL, max_pages)
        ]
        ml = ml_ref[r]
        state = (ml[:, 0:1], ml[:, 1:2], a_ref[r])
        _, total, accum = merge([state] + page_blocks(q_all, pages, LOCAL, len_ref[r]))
        att = (accum / total).astype(att_sc.dtype)
        for g in range(heads):
            att_sc[rows, pl.ds(g * HEAD_SIZE, HEAD_SIZE)] = att[g * tree_len : (g + 1) * tree_len]

    weight_copy.wait()
    proj_ref[...] = jnp.dot(
        att_sc[...], weight_vmem[...], preferred_element_type=jnp.float32
    ).astype(proj_ref.dtype)


def step(queries, tree_kv, page_pool, page_table, cache_len, parents, accepted, o_weight):
    requests, tree_len = parents.shape
    heads = queries.shape[1] // HEAD_SIZE
    pool_slots = page_pool[:, 0]
    own_slots = requests * LOCAL
    ring = lax.axis_size("req")
    spill_source = pool_slots[own_slots:]
    spill = lax.ppermute(spill_source, "req", [((i + 1) % ring, i) for i in range(ring)])
    tree_rows = tree_kv[:, 0, :]
    smem = pl.BlockSpec(memory_space=pltpu.SMEM)
    vmem = pl.BlockSpec(memory_space=pltpu.VMEM)
    stacked = heads * tree_len
    local_call = pl.pallas_call(
        local_kernel,
        out_shape=(
            jax.ShapeDtypeStruct(tree_rows.shape, jnp.bfloat16),
            jax.ShapeDtypeStruct((requests, stacked, HEAD_SIZE), jnp.float32),
            jax.ShapeDtypeStruct((requests, stacked, HEAD_SIZE), jnp.float32),
            jax.ShapeDtypeStruct((requests, stacked, HEAD_SIZE), jnp.bfloat16),
        ),
        in_specs=[smem, smem, smem, vmem, vmem, vmem, vmem],
        out_specs=(vmem, vmem, vmem, vmem),
    )
    kept, packed, accum, stacked_q = local_call(
        page_table, cache_len, accepted, parents, queries, tree_rows, pool_slots
    )
    partial = pl.pallas_call(
        functools.partial(spill_kernel, own_slots),
        out_shape=jax.ShapeDtypeStruct((queries.shape[0], o_weight.shape[1]), jnp.bfloat16),
        in_specs=[smem, smem, vmem, vmem, vmem, vmem, pl.BlockSpec(memory_space=pl.ANY)],
        out_specs=vmem,
        scratch_shapes=[
            pltpu.VMEM(o_weight.shape, o_weight.dtype),
            pltpu.VMEM(queries.shape, jnp.bfloat16),
            pltpu.SemaphoreType.DMA(()),
        ],
    )(page_table, cache_len, packed, accum, stacked_q, spill, o_weight)

    parts = lax.axis_size("tp")
    gathered = lax.all_to_all(partial, "tp", 0, 0, tiled=True)
    blocks = gathered.reshape(parts, partial.shape[0] // parts, partial.shape[1])
    summed = blocks[0].astype(jnp.float32)
    for i in range(1, parts):
        summed = summed + blocks[i].astype(jnp.float32)
    projected = summed.astype(jnp.bfloat16)
    return (projected, kept.reshape(kept.shape[0], 1, kept.shape[1]))


def solution(mesh):
    in_specs = (
        P("req", "tp"),
        P("req", "tp", None),
        P("req", "tp", None, None),
        P("req", None),
        P("req"),
        P("req", None),
        P("req"),
        P("tp", None),
    )
    out_specs = (P(("req", "tp"), None), P("req", "tp", None))
    return jax.shard_map(step, mesh=mesh, in_specs=in_specs, out_specs=out_specs, check_vma=False)
```

```python
import functools
import math

import jax
import jax.numpy as jnp
from jax import lax
from jax.experimental import pallas as pl
from jax.experimental.pallas import tpu as pltpu
from jax.sharding import PartitionSpec as P

HEAD_SIZE = 128
LOCAL = 2

very_negative = -1e30


def nt_dot(a, b):
    return lax.dot_general(a, b, (((1,), (1,)), ((), ())), preferred_element_type=jnp.float32)


def stacked_queries(q_ref, rows, heads):
    q = q_ref[rows, :]
    return jnp.concatenate(
        [q[:, g * HEAD_SIZE : (g + 1) * HEAD_SIZE] for g in range(heads)], axis=0
    )


def page_blocks(q_all, pages, first_page, length):
    page_len = pages[0].shape[0]
    keys = jnp.concatenate([page[:, :HEAD_SIZE] for page in pages], axis=0)
    lane = lax.broadcasted_iota(jnp.int32, (1, keys.shape[0]), 1)
    visible = (first_page * page_len + lane) < length
    scores = nt_dot(q_all, keys) * (1.0 / math.sqrt(HEAD_SIZE))
    scores = jnp.where(visible, scores, very_negative)
    blocks = []
    for k, page in enumerate(pages):
        cols = slice(k * page_len, (k + 1) * page_len)
        s = scores[:, cols]
        m = jnp.max(s, axis=1, keepdims=True)
        w = jnp.exp(s - m).astype(jnp.bfloat16)
        l = jnp.sum(w.astype(jnp.float32), axis=1, keepdims=True)
        a = jnp.dot(w, page[:, HEAD_SIZE:], preferred_element_type=jnp.float32)
        blocks.append((m, l, a))
    return blocks


def merge(blocks):
    top = blocks[0][0]
    for m, _, _ in blocks[1:]:
        top = jnp.maximum(top, m)
    total = None
    accum = None
    for m, l, a in blocks:
        f = jnp.exp(m - top)
        total = f * l if total is None else total + f * l
        accum = f * a if accum is None else accum + f * a
    return top, total, accum


def local_kernel(
    table_ref, len_ref, leaf_ref, parents_ref, q_ref, tree_ref, pool_ref,
    kept_ref, ml_ref, a_ref, qs_ref,
):
    n_req, tree_len = parents_ref.shape
    nodes = n_req * tree_len
    heads = q_ref.shape[1] // HEAD_SIZE
    stacked = heads * tree_len
    scale = 1.0 / math.sqrt(HEAD_SIZE)
    sub = lax.broadcasted_iota(jnp.int32, (nodes, nodes), 0)
    lane = lax.broadcasted_iota(jnp.int32, (nodes, nodes), 1)
    eye = (sub == lane).astype(jnp.float32)
    squarings = (tree_len - 1).bit_length()

    parents = parents_ref[...].astype(jnp.float32)
    first = lax.broadcasted_iota(jnp.int32, parents.shape, 0).astype(jnp.float32) * tree_len
    parents = jnp.where(parents >= 0.0, parents + first, -1.0).astype(jnp.bfloat16)
    node = lax.broadcasted_iota(jnp.int32, (tree_len, nodes), 0)
    column = lax.broadcasted_iota(jnp.int32, (tree_len, nodes), 1)
    parent_row = None
    for r in range(n_req):
        place = (column == node + r * tree_len).astype(jnp.bfloat16)
        lhs = jnp.broadcast_to(parents[r : r + 1], (16, tree_len))
        placed = jnp.dot(lhs, place, preferred_element_type=jnp.float32)[0:1]
        parent_row = placed if parent_row is None else parent_row + placed

    rt = eye + (sub.astype(jnp.float32) == parent_row).astype(jnp.float32)
    for _ in range(squarings):
        rb = rt.astype(jnp.bfloat16)
        rt = jnp.minimum(jnp.dot(rb, rb, preferred_element_type=jnp.float32), 1.0)
    reach = nt_dot(eye.astype(jnp.bfloat16), rt.astype(jnp.bfloat16))

    depth = jnp.sum(rt, axis=0, keepdims=True) - 1.0
    slot = lax.broadcasted_iota(jnp.int32, (tree_len, nodes), 0).astype(jnp.float32)
    selectors = []
    for r in range(n_req):
        leaf = r * tree_len + leaf_ref[r]
        kept_mask = jnp.sum(jnp.where(sub == leaf, reach, 0.0), axis=0, keepdims=True)
        selectors.append(jnp.where((slot == depth) & (kept_mask > 0.5), 1.0, 0.0))
    selector = jnp.concatenate(selectors, axis=0).astype(jnp.bfloat16)
    tree_rows = tree_ref[...]
    kept_ref[...] = jnp.dot(selector, tree_rows, preferred_element_type=jnp.float32).astype(
        kept_ref.dtype
    )

    q_all = [stacked_queries(q_ref, pl.ds(r * tree_len, tree_len), heads) for r in range(n_req)]
    for r in range(n_req):
        qs_ref[r] = q_all[r]
    tree_mask = (
        jnp.concatenate(
            [reach[r * tree_len : (r + 1) * tree_len] for r in range(n_req) for _ in range(heads)],
            axis=0,
        )
        > 0.5
    )
    s = nt_dot(jnp.concatenate(q_all, axis=0), tree_rows[:, :HEAD_SIZE]) * scale
    s = jnp.where(tree_mask, s, very_negative)
    m = jnp.max(s, axis=1, keepdims=True)
    w = jnp.exp(s - m).astype(jnp.bfloat16)
    l = jnp.sum(w.astype(jnp.float32), axis=1, keepdims=True)
    a = jnp.dot(w, tree_rows[:, HEAD_SIZE:], preferred_element_type=jnp.float32)

    state_lane = lax.broadcasted_iota(jnp.int32, (stacked, HEAD_SIZE), 1)
    for r in range(n_req):
        rows = slice(r * stacked, (r + 1) * stacked)
        pages = [pool_ref[table_ref[r, k]] for k in range(LOCAL)]
        blocks = [(m[rows], l[rows], a[rows])] + page_blocks(q_all[r], pages, 0, len_ref[r])
        top, total, accum = merge(blocks)
        ml_ref[r] = jnp.where(state_lane == 0, top, jnp.where(state_lane == 1, total, 0.0))
        a_ref[r] = accum


def spill_kernel(
    spill_base, table_ref, len_ref, ml_ref, a_ref, q_ref, spill_ref, weight_hbm,
    proj_ref, weight_vmem, att_sc, weight_sem,
):
    weight_copy = pltpu.make_async_copy(weight_hbm, weight_vmem, weight_sem)
    weight_copy.start()
    n_req, tree_len = table_ref.shape[0], att_sc.shape[0] // table_ref.shape[0]
    heads = att_sc.shape[1] // HEAD_SIZE
    max_pages = table_ref.shape[1]
    spill_slots = spill_ref.shape[0]
    for r in range(n_req):
        rows = pl.ds(r * tree_len, tree_len)
        q_all = q_ref[r]
        pages = [
            spill_ref[jnp.clip(table_ref[r, k] - spill_base, 0, spill_slots - 1)]
            for k in range(LOCAL, max_pages)
        ]
        ml = ml_ref[r]
        state = (ml[:, 0:1], ml[:, 1:2], a_ref[r])
        _, total, accum = merge([state] + page_blocks(q_all, pages, LOCAL, len_ref[r]))
        att = (accum / total).astype(att_sc.dtype)
        for g in range(heads):
            att_sc[rows, pl.ds(g * HEAD_SIZE, HEAD_SIZE)] = att[g * tree_len : (g + 1) * tree_len]

    weight_copy.wait()
    proj_ref[...] = jnp.dot(
        att_sc[...], weight_vmem[...], preferred_element_type=jnp.float32
    ).astype(proj_ref.dtype)


def step(queries, tree_kv, page_pool, page_table, cache_len, parents, accepted, o_weight):
    requests, tree_len = parents.shape
    heads = queries.shape[1] // HEAD_SIZE
    pool_slots = page_pool[:, 0]
    own_slots = requests * LOCAL
    ring = lax.axis_size("req")
    spill_source = pool_slots[own_slots:]
    spill = lax.ppermute(spill_source, "req", [((i + 1) % ring, i) for i in range(ring)])
    tree_rows = tree_kv[:, 0, :]
    smem = pl.BlockSpec(memory_space=pltpu.SMEM)
    vmem = pl.BlockSpec(memory_space=pltpu.VMEM)
    stacked = heads * tree_len
    local_call = pl.pallas_call(
        local_kernel,
        out_shape=(
            jax.ShapeDtypeStruct(tree_rows.shape, jnp.bfloat16),
            jax.ShapeDtypeStruct((requests, stacked, HEAD_SIZE), jnp.float32),
            jax.ShapeDtypeStruct((requests, stacked, HEAD_SIZE), jnp.float32),
            jax.ShapeDtypeStruct((requests, stacked, HEAD_SIZE), jnp.bfloat16),
        ),
        in_specs=[smem, smem, smem, vmem, vmem, vmem, vmem],
        out_specs=(vmem, vmem, vmem, vmem),
    )
    kept, packed, accum, stacked_q = local_call(
        page_table, cache_len, accepted, parents, queries, tree_rows, pool_slots
    )
    partial = pl.pallas_call(
        functools.partial(spill_kernel, own_slots),
        out_shape=jax.ShapeDtypeStruct((queries.shape[0], o_weight.shape[1]), jnp.bfloat16),
        in_specs=[smem, smem, vmem, vmem, vmem, vmem, pl.BlockSpec(memory_space=pl.ANY)],
        out_specs=vmem,
        scratch_shapes=[
            pltpu.VMEM(o_weight.shape, o_weight.dtype),
            pltpu.VMEM(queries.shape, jnp.bfloat16),
            pltpu.SemaphoreType.DMA(()),
        ],
    )(
        page_table, cache_len, packed, accum, stacked_q,
        pltpu.with_memory_space_constraint(spill, pltpu.MemorySpace.VMEM), o_weight,
    )

    parts = lax.axis_size("tp")
    gathered = lax.all_to_all(partial, "tp", 0, 0, tiled=True)
    blocks = gathered.reshape(parts, partial.shape[0] // parts, partial.shape[1])
    summed = blocks[0].astype(jnp.float32)
    for i in range(1, parts):
        summed = summed + blocks[i].astype(jnp.float32)
    projected = summed.astype(jnp.bfloat16)
    return (projected, kept.reshape(kept.shape[0], 1, kept.shape[1]))


def solution(mesh):
    in_specs = (
        P("req", "tp"),
        P("req", "tp", None),
        P("req", "tp", None, None),
        P("req", None),
        P("req"),
        P("req", None),
        P("req"),
        P("tp", None),
    )
    out_specs = (P(("req", "tp"), None), P("req", "tp", None))
    return jax.shard_map(step, mesh=mesh, in_specs=in_specs, out_specs=out_specs, check_vma=False)
```

```python
import functools
import math

import jax
import jax.numpy as jnp
from jax import lax
from jax.experimental import pallas as pl
from jax.experimental.pallas import tpu as pltpu
from jax.sharding import PartitionSpec as P

HEAD_SIZE = 128
LOCAL = 2

very_negative = -1e30


def nt_dot(a, b):
    return lax.dot_general(a, b, (((1,), (1,)), ((), ())), preferred_element_type=jnp.float32)


def stacked_queries(q_ref, rows, heads):
    q = q_ref[rows, :]
    return jnp.concatenate(
        [q[:, g * HEAD_SIZE : (g + 1) * HEAD_SIZE] for g in range(heads)], axis=0
    )


def page_blocks(q_all, pages, first_page, length):
    page_len = pages[0].shape[0]
    keys = jnp.concatenate([page[:, :HEAD_SIZE] for page in pages], axis=0)
    lane = lax.broadcasted_iota(jnp.int32, (1, keys.shape[0]), 1)
    visible = (first_page * page_len + lane) < length
    scores = nt_dot(q_all, keys) * (1.0 / math.sqrt(HEAD_SIZE))
    scores = jnp.where(visible, scores, very_negative)
    blocks = []
    for k, page in enumerate(pages):
        cols = slice(k * page_len, (k + 1) * page_len)
        s = scores[:, cols]
        m = jnp.max(s, axis=1, keepdims=True)
        w = jnp.exp(s - m).astype(jnp.bfloat16)
        l = jnp.sum(w.astype(jnp.float32), axis=1, keepdims=True)
        a = jnp.dot(w, page[:, HEAD_SIZE:], preferred_element_type=jnp.float32)
        blocks.append((m, l, a))
    return blocks


def merge(blocks):
    top = blocks[0][0]
    for m, _, _ in blocks[1:]:
        top = jnp.maximum(top, m)
    total = None
    accum = None
    for m, l, a in blocks:
        f = jnp.exp(m - top)
        total = f * l if total is None else total + f * l
        accum = f * a if accum is None else accum + f * a
    return top, total, accum


def local_kernel(
    table_ref, len_ref, leaf_ref, parents_ref, q_ref, tree_ref, pool_ref,
    kept_ref, ml_ref, a_ref, qs_ref,
):
    n_req, tree_len = parents_ref.shape
    nodes = n_req * tree_len
    heads = q_ref.shape[1] // HEAD_SIZE
    stacked = heads * tree_len
    scale = 1.0 / math.sqrt(HEAD_SIZE)
    sub = lax.broadcasted_iota(jnp.int32, (nodes, nodes), 0)
    lane = lax.broadcasted_iota(jnp.int32, (nodes, nodes), 1)
    eye = (sub == lane).astype(jnp.float32)
    squarings = (tree_len - 1).bit_length()

    parents = parents_ref[...].astype(jnp.float32)
    first = lax.broadcasted_iota(jnp.int32, parents.shape, 0).astype(jnp.float32) * tree_len
    parents = jnp.where(parents >= 0.0, parents + first, -1.0).astype(jnp.bfloat16)
    node = lax.broadcasted_iota(jnp.int32, (tree_len, nodes), 0)
    column = lax.broadcasted_iota(jnp.int32, (tree_len, nodes), 1)
    parent_row = None
    for r in range(n_req):
        place = (column == node + r * tree_len).astype(jnp.bfloat16)
        lhs = jnp.broadcast_to(parents[r : r + 1], (16, tree_len))
        placed = jnp.dot(lhs, place, preferred_element_type=jnp.float32)[0:1]
        parent_row = placed if parent_row is None else parent_row + placed

    rt = eye + (sub.astype(jnp.float32) == parent_row).astype(jnp.float32)
    for _ in range(squarings):
        rb = rt.astype(jnp.bfloat16)
        rt = jnp.minimum(jnp.dot(rb, rb, preferred_element_type=jnp.float32), 1.0)
    reach = nt_dot(eye.astype(jnp.bfloat16), rt.astype(jnp.bfloat16))

    depth = jnp.sum(rt, axis=0, keepdims=True) - 1.0
    slot = lax.broadcasted_iota(jnp.int32, (tree_len, nodes), 0).astype(jnp.float32)
    selectors = []
    for r in range(n_req):
        leaf = r * tree_len + leaf_ref[r]
        kept_mask = jnp.sum(jnp.where(sub == leaf, reach, 0.0), axis=0, keepdims=True)
        selectors.append(jnp.where((slot == depth) & (kept_mask > 0.5), 1.0, 0.0))
    selector = jnp.concatenate(selectors, axis=0).astype(jnp.bfloat16)
    tree_rows = tree_ref[...]
    kept_ref[...] = jnp.dot(selector, tree_rows, preferred_element_type=jnp.float32).astype(
        kept_ref.dtype
    )

    q_all = [stacked_queries(q_ref, pl.ds(r * tree_len, tree_len), heads) for r in range(n_req)]
    for r in range(n_req):
        qs_ref[r] = q_all[r]
    tree_mask = (
        jnp.concatenate(
            [reach[r * tree_len : (r + 1) * tree_len] for r in range(n_req) for _ in range(heads)],
            axis=0,
        )
        > 0.5
    )
    s = nt_dot(jnp.concatenate(q_all, axis=0), tree_rows[:, :HEAD_SIZE]) * scale
    s = jnp.where(tree_mask, s, very_negative)
    m = jnp.max(s, axis=1, keepdims=True)
    w = jnp.exp(s - m).astype(jnp.bfloat16)
    l = jnp.sum(w.astype(jnp.float32), axis=1, keepdims=True)
    a = jnp.dot(w, tree_rows[:, HEAD_SIZE:], preferred_element_type=jnp.float32)

    state_lane = lax.broadcasted_iota(jnp.int32, (stacked, HEAD_SIZE), 1)
    for r in range(n_req):
        rows = slice(r * stacked, (r + 1) * stacked)
        pages = [pool_ref[table_ref[r, k]] for k in range(LOCAL)]
        blocks = [(m[rows], l[rows], a[rows])] + page_blocks(q_all[r], pages, 0, len_ref[r])
        top, total, accum = merge(blocks)
        ml_ref[r] = jnp.where(state_lane == 0, top, jnp.where(state_lane == 1, total, 0.0))
        a_ref[r] = accum


def spill_kernel(
    spill_base, table_ref, len_ref, ml_ref, a_ref, q_ref, spill_ref, weight_hbm,
    proj_ref, weight_vmem, att_sc, weight_sem,
):
    weight_copy = pltpu.make_async_copy(weight_hbm, weight_vmem, weight_sem)
    weight_copy.start()
    n_req, tree_len = table_ref.shape[0], att_sc.shape[0] // table_ref.shape[0]
    heads = att_sc.shape[1] // HEAD_SIZE
    max_pages = table_ref.shape[1]
    spill_slots = spill_ref.shape[0]
    for r in range(n_req):
        rows = pl.ds(r * tree_len, tree_len)
        q_all = q_ref[r]
        pages = [
            spill_ref[jnp.clip(table_ref[r, k] - spill_base, 0, spill_slots - 1)]
            for k in range(LOCAL, max_pages)
        ]
        ml = ml_ref[r]
        state = (ml[:, 0:1], ml[:, 1:2], a_ref[r])
        _, total, accum = merge([state] + page_blocks(q_all, pages, LOCAL, len_ref[r]))
        att = (accum / total).astype(att_sc.dtype)
        for g in range(heads):
            att_sc[rows, pl.ds(g * HEAD_SIZE, HEAD_SIZE)] = att[g * tree_len : (g + 1) * tree_len]

    weight_copy.wait()
    proj_ref[...] = jnp.dot(
        att_sc[...], weight_vmem[...], preferred_element_type=jnp.float32
    ).astype(proj_ref.dtype)


def step(queries, tree_kv, page_pool, page_table, cache_len, parents, accepted, o_weight):
    requests, tree_len = parents.shape
    heads = queries.shape[1] // HEAD_SIZE
    pool_slots = page_pool[:, 0]
    own_slots = requests * LOCAL
    ring = lax.axis_size("req")
    spill_source = pool_slots[own_slots:]
    spill = lax.ppermute(spill_source, "req", [((i + 1) % ring, i) for i in range(ring)])
    tree_rows = tree_kv[:, 0, :]
    smem = pl.BlockSpec(memory_space=pltpu.SMEM)
    vmem = pl.BlockSpec(memory_space=pltpu.VMEM)
    stacked = heads * tree_len
    local_call = pl.pallas_call(
        local_kernel,
        out_shape=(
            jax.ShapeDtypeStruct(tree_rows.shape, jnp.bfloat16),
            jax.ShapeDtypeStruct((requests, stacked, HEAD_SIZE), jnp.float32),
            jax.ShapeDtypeStruct((requests, stacked, HEAD_SIZE), jnp.float32),
            jax.ShapeDtypeStruct((requests, stacked, HEAD_SIZE), jnp.bfloat16),
        ),
        in_specs=[smem, smem, smem, vmem, vmem, vmem, vmem],
        out_specs=(vmem, vmem, vmem, vmem),
    )
    kept, packed, accum, stacked_q = local_call(
        page_table, cache_len, accepted, parents, queries, tree_rows, pool_slots
    )
    partial = pl.pallas_call(
        functools.partial(spill_kernel, own_slots),
        out_shape=jax.ShapeDtypeStruct((queries.shape[0], o_weight.shape[1]), jnp.bfloat16),
        in_specs=[smem, smem, vmem, vmem, vmem, vmem, pl.BlockSpec(memory_space=pl.ANY)],
        out_specs=vmem,
        scratch_shapes=[
            pltpu.VMEM(o_weight.shape, o_weight.dtype),
            pltpu.VMEM(queries.shape, jnp.bfloat16),
            pltpu.SemaphoreType.DMA(()),
        ],
    )(
        page_table, cache_len,
        *[pltpu.with_memory_space_constraint(x, pltpu.MemorySpace.VMEM)
          for x in (packed, accum, stacked_q, spill)],
        o_weight,
    )

    parts = lax.axis_size("tp")
    gathered = lax.all_to_all(partial, "tp", 0, 0, tiled=True)
    blocks = gathered.reshape(parts, partial.shape[0] // parts, partial.shape[1])
    summed = blocks[0].astype(jnp.float32)
    for i in range(1, parts):
        summed = summed + blocks[i].astype(jnp.float32)
    projected = summed.astype(jnp.bfloat16)
    return (projected, kept.reshape(kept.shape[0], 1, kept.shape[1]))


def solution(mesh):
    in_specs = (
        P("req", "tp"),
        P("req", "tp", None),
        P("req", "tp", None, None),
        P("req", None),
        P("req"),
        P("req", None),
        P("req"),
        P("tp", None),
    )
    out_specs = (P(("req", "tp"), None), P("req", "tp", None))
    return jax.shard_map(step, mesh=mesh, in_specs=in_specs, out_specs=out_specs, check_vma=False)
```
